256 devices in a mesh: heads: 32 (over z_hi, y, x), width: 8 (over z_lo, core).
Axes of the slice: x: 4, y: 4, z: 8 (z_hi: 2, z_lo: 4; z = z_hi * 4 + z_lo), core: 2. Of those that a mesh axis runs over, the one named last changes fastest.
Arguments:
- states: bfloat16 [1536, 6144], P('heads', 'width'), may hold values from -6 to 6
- segment_ids: int32 [1536], replicated, may hold values from 0 to 11, never falling along the last dimension, each value on 1 to 1344 neighbouring positions
- attn_gain: float32 [6144], P('width'), may hold values from 0.1 to 1.9
- attn_shift: float32 [6144], P('width'), may hold values from -3 to 3
- mlp_gain: float32 [6144], P('width'), may hold values from 0.1 to 1.9
- mlp_shift: float32 [6144], P('width'), may hold values from -3 to 3
- qkv_weight: bfloat16 [6144, 18432], P('width', 'heads'), may hold values from -0.078125 to 0.078125
- qkv_bias: float32 [18432], P('heads'), may hold values from -6 to 6
- dense_weight: bfloat16 [6144, 6144], P('heads', 'width'), may hold values from -0.078125 to 0.078125
- dense_bias: float32 [6144], P('width'), may hold values from -2 to 2
- up_weight: bfloat16 [6144, 24576], P('width', 'heads'), may hold values from -0.078125 to 0.078125
- up_bias: float32 [24576], P('heads'), may hold values from -3 to 3
- down_weight: bfloat16 [24576, 6144], P('heads', 'width'), may hold values from -0.0390625 to 0.0390625
- down_bias: float32 [6144], P('width'), may hold values from -2 to 2
Outputs:
- layer_out: bfloat16 [1536, 6144], P('heads', 'width')
- key_cache: bfloat16 [1536, 6144], P('width', 'heads')
- value_cache: bfloat16 [1536, 6144], P('width', 'heads')
The draws below stay inside these ranges and needn't reach their ends.
Inputs may be any that keep to these rules, and one draw needn't show every extreme that they name: `segment_ids`: document numbers never fall along the tokens; each document has 1 to 1344 tokens and one has exactly 1344.
All inputs are finite; a program needn't handle non-finite values.
Results may differ from the reference program's by a relative error of at most 0.017.
Values may be sent and summed in bfloat16 or wider, within the bound.
No kernel may reach another device: no remote copies, remote signals or barrier semaphores. Data moves between devices by JAX's collectives and lax.ppermute only.
A program may use at most 64 MiB of HBM per device.

```python
import math
import jax
import jax.numpy as jnp
import numpy as np
from jax import lax

NH = 64
HD = 96
ROT = 24
FF = 24576
D = 6144
TOKENS = 1536
MAX_LEN = 1344
SEGS = 12


planted_scale = 6.0


def draw_qkv_bias(key, part):
    base_key = jax.random.fold_in(key, 11)
    head_key = jax.random.fold_in(key, 12)
    sign_key = jax.random.fold_in(key, 13)
    background = jnp.clip(0.5 * jax.random.normal(base_key, (NH, 3, HD), jnp.float32), -3.0, 3.0)
    shuffled = jax.random.permutation(head_key, NH)
    levels = jnp.zeros((NH,), jnp.float32).at[shuffled[:3]].set(jnp.array([1.0, 0.85, 0.7], jnp.float32))
    sign_flip = jnp.where(jax.random.bernoulli(sign_key, 0.5, (NH, HD)), 1.0, -1.0).astype(jnp.float32)
    head_dims = jnp.arange(HD, dtype=jnp.int32)
    sign_flip = jnp.where(head_dims[None, :] == ROT, 1.0, jnp.where(head_dims[None, :] == ROT + 1, -1.0, sign_flip)).astype(jnp.float32)
    planted = planted_scale * levels[:, None] * sign_flip
    chosen = (head_dims[None, :] >= ROT) & (levels[:, None] > 0.0)
    query_key = jnp.arange(3, dtype=jnp.int32)[None, :, None] < 2
    planted_mask = chosen[:, None, :] & query_key
    result = jnp.where(planted_mask, planted[:, None, :], background)
    return result.reshape(3 * NH * HD).astype(jnp.float32)


def level_of(own_key, shape, shards, low, largest):
    gain, own = 1.0, jax.random.fold_in(own_key, 6)
    for dim, parts in shards:
        steps = jnp.exp(jax.random.uniform(jax.random.fold_in(own, dim), (parts,), jnp.float32, low / len(shards), largest / len(shards)))
        gain = gain * jnp.repeat(steps, shape[dim] // parts).reshape([-1 if axis == dim else 1 for axis in range(len(shape))])
    return gain


def split_up(number_of, total, bound, slope):
    weights = [(1 << 20) // math.isqrt(rank ** slope) + 1 for rank in range(2, number_of + 1)]
    spare, counts = total - bound - (number_of - 1), [1] * (number_of - 1)
    while spare > 0:
        movable = [i for i in range(number_of - 1) if counts[i] < bound]
        pool, budget = sum([weights[i] for i in movable]), spare
        for i in movable:
            addition = min(bound - counts[i], max(1, budget * weights[i] // pool), spare)
            counts[i] = counts[i] + addition
            spare = spare - addition
    return np.array([bound] + counts)


def ragged_sizes(stream_key, number_of, total, bound, lean):
    if number_of == 2:
        one = jax.random.randint(stream_key, (), max(1, total - bound), min(bound, total - 1) + 1)
        return jnp.stack([one, total - one])
    tallies = jnp.asarray(split_up(number_of, total, bound, lean), jnp.int32)
    couples = (number_of - 1) // 2
    giver, sink = tallies[1:1 + 2 * couples:2], tallies[2:2 + 2 * couples:2]
    margin = jnp.minimum(giver - 1, bound - sink)
    passed = jax.random.randint(jax.random.fold_in(stream_key, 1), (couples,), 0, 1 << 20) % (margin + 1)
    tallies = tallies.at[1:1 + 2 * couples:2].set(giver - passed).at[2:2 + 2 * couples:2].set(sink + passed)
    return tallies[jax.random.permutation(jax.random.fold_in(stream_key, 2), number_of)]


def normal_values(stream_key, extent, width, most, pieces=(), kind=jnp.bfloat16):
    values = jax.random.normal(stream_key, extent, jnp.float32) * width
    if len(pieces) > 0:
        values = level_of(stream_key, extent, pieces, -0.22, 0.18) * values
    return jnp.clip(values, min=-most, max=most).astype(kind)


def setup_inputs(seed: int = 0) -> dict:
    key_of = jax.random.split(jax.random.key(seed), 15)
    states = normal_values(key_of[0], (TOKENS, D), 1.0, 6.0, ((0, 32), (1, 8)))
    segment_ids = jnp.searchsorted(jnp.cumsum(ragged_sizes(key_of[1], SEGS, TOKENS, MAX_LEN, 0)), jnp.arange(TOKENS), side="right").astype(jnp.int32)
    attn_gain = jnp.clip(1.0 + 0.18 * jax.random.normal(key_of[2], (D,), jnp.float32), 0.1, 1.9)
    attn_shift = normal_values(key_of[3], (D,), 0.5, 3.0, ((0, 8),), jnp.float32)
    mlp_gain = jnp.clip(1.0 + 0.18 * jax.random.normal(key_of[4], (D,), jnp.float32), 0.1, 1.9)
    mlp_shift = normal_values(key_of[5], (D,), 0.5, 3.0, ((0, 8),), jnp.float32)
    qkv_weight = normal_values(key_of[6], (D, 3 * D), D ** -0.5, 0.078125, ((0, 8), (1, 32)))
    qkv_bias = draw_qkv_bias(jax.random.fold_in(key_of[14], 71), 0)
    dense_weight = normal_values(key_of[8], (D, D), D ** -0.5, 0.078125, ((0, 32), (1, 8)))
    dense_bias = normal_values(key_of[9], (D,), 0.3, 2.0, ((0, 8),), jnp.float32)
    up_weight = normal_values(key_of[10], (D, FF), D ** -0.5, 0.078125, ((0, 8), (1, 32)))
    up_bias = normal_values(key_of[11], (FF,), 0.5, 3.0, ((0, 32),), jnp.float32)
    down_weight = normal_values(key_of[12], (FF, D), FF ** -0.5, 0.0390625, ((0, 32), (1, 8)))
    down_bias = normal_values(key_of[13], (D,), 0.3, 2.0, ((0, 8),), jnp.float32)
    return {"states": states, "segment_ids": segment_ids, "attn_gain": attn_gain, "attn_shift": attn_shift, "mlp_gain": mlp_gain, "mlp_shift": mlp_shift, "qkv_weight": qkv_weight, "qkv_bias": qkv_bias, "dense_weight": dense_weight, "dense_bias": dense_bias, "up_weight": up_weight, "up_bias": up_bias, "down_weight": down_weight, "down_bias": down_bias}


norm_epsilon = 1e-05

def positions_of(segments):
    count = segments.shape[0]
    row_index = jnp.arange(count, dtype=jnp.int32)
    change = jnp.concatenate([jnp.ones((1,), bool), segments[1:] != segments[:-1]])
    first = lax.cummax(jnp.where(change, row_index, 0).astype(jnp.int32), axis=0)
    return (row_index - first).astype(jnp.float32)

def rotary(values, positions):
    half_rot = ROT // 2
    inverse = 10000.0 ** (-(jnp.arange(half_rot, dtype=jnp.float32) * 2.0 / ROT))
    angles = positions[:, None] * inverse[None, :]
    cosine = jnp.cos(angles)[:, None, :]
    sine_part = jnp.sin(angles)[:, None, :]
    first_half = values[..., :half_rot]
    second_half = values[..., half_rot:ROT]
    return jnp.concatenate([first_half * cosine - second_half * sine_part, second_half * cosine + first_half * sine_part, values[..., ROT:]], axis=-1)

def reference(states, segment_ids, attn_gain, attn_shift, mlp_gain, mlp_shift, qkv_weight, qkv_bias, dense_weight, dense_bias, up_weight, up_bias, down_weight, down_bias):
    floats = states.astype(jnp.float32)
    row_mean = lax.optimization_barrier(jnp.sum(floats, -1, keepdims=True)) / D
    row_var = lax.optimization_barrier(jnp.sum(floats * floats, -1, keepdims=True)) / D - row_mean * row_mean
    normed = ((floats - row_mean) * lax.rsqrt(row_var + norm_epsilon)).astype(jnp.bfloat16)
    normed_f = normed.astype(jnp.float32)
    attn_in = (normed_f * attn_gain + attn_shift).astype(jnp.bfloat16)
    mlp_in = (normed_f * mlp_gain + mlp_shift).astype(jnp.bfloat16)
    qkv = jnp.dot(attn_in, qkv_weight, preferred_element_type=jnp.float32) + qkv_bias
    qkv = qkv.reshape(TOKENS, NH, 3, HD)
    positions = positions_of(segment_ids)
    queries = rotary(qkv[:, :, 0, :], positions).astype(jnp.bfloat16)
    keys_all = rotary(qkv[:, :, 1, :], positions).astype(jnp.bfloat16)
    values_all = qkv[:, :, 2, :].astype(jnp.bfloat16)
    row_index = jnp.arange(TOKENS, dtype=jnp.int32)
    allowed = (segment_ids[:, None] == segment_ids[None, :]) & (row_index[None, :] <= row_index[:, None])
    score_scale = 1.0 / HD ** 0.5

    def one_head(inputs):
        head_q, head_k, head_v = inputs
        scores = jnp.dot(head_q, head_k.T, preferred_element_type=jnp.float32) * score_scale
        scores = jnp.where(allowed, scores, -1e+30)
        top = lax.optimization_barrier(jnp.max(scores, -1, keepdims=True))
        weights = jnp.where(allowed, jnp.exp(scores - top), 0.0)
        total = lax.optimization_barrier(jnp.sum(weights, -1, keepdims=True))
        mixed = jnp.dot(weights.astype(jnp.bfloat16), head_v, preferred_element_type=jnp.float32)
        return (mixed / total).astype(jnp.bfloat16)
    attended = lax.map(one_head, (queries.transpose(1, 0, 2), keys_all.transpose(1, 0, 2), values_all.transpose(1, 0, 2)))
    attended = attended.transpose(1, 0, 2).reshape(TOKENS, D)
    attn_out = jnp.dot(attended, dense_weight, preferred_element_type=jnp.float32)
    hidden = jax.nn.gelu(jnp.dot(mlp_in, up_weight, preferred_element_type=jnp.float32) + up_bias, approximate=False).astype(jnp.bfloat16)
    mlp_out = jnp.dot(hidden, down_weight, preferred_element_type=jnp.float32)
    layer_out = (floats + attn_out + mlp_out + dense_bias + down_bias).astype(jnp.bfloat16)
    return (layer_out, keys_all.reshape(TOKENS, D), values_all.reshape(TOKENS, D))
```

```python
import jax
import jax.numpy as jnp
from jax import lax
from jax.sharding import PartitionSpec as P

HD = 96
ROT = 24
D = 6144


norm_epsilon = 1e-05


def positions_of(segments):
    count = segments.shape[0]
    row_index = jnp.arange(count, dtype=jnp.int32)
    change = jnp.concatenate([jnp.ones((1,), bool), segments[1:] != segments[:-1]])
    first = lax.cummax(jnp.where(change, row_index, 0), axis=0)
    return (row_index - first).astype(jnp.float32)


def rotary(values, positions):
    half_rot = ROT // 2
    inverse = 10000.0 ** (-(jnp.arange(half_rot, dtype=jnp.float32) * 2.0 / ROT))
    angles = positions[:, None] * inverse[None, :]
    cosine = jnp.cos(angles)[:, None, :]
    sine_part = jnp.sin(angles)[:, None, :]
    first_half = values[..., :half_rot]
    second_half = values[..., half_rot:ROT]
    return jnp.concatenate(
        [
            first_half * cosine - second_half * sine_part,
            second_half * cosine + first_half * sine_part,
            values[..., ROT:],
        ],
        axis=-1,
    )


def on_device(
    states,
    segment_ids,
    attn_gain,
    attn_shift,
    mlp_gain,
    mlp_shift,
    qkv_weight,
    qkv_bias,
    dense_weight,
    dense_bias,
    up_weight,
    up_bias,
    down_weight,
    down_bias,
):
    floats = states.astype(jnp.float32)
    row_sums, square_sums = lax.psum((jnp.sum(floats, -1), jnp.sum(floats * floats, -1)), "width")
    row_mean = (row_sums / D)[:, None]
    row_var = (square_sums / D)[:, None] - row_mean * row_mean
    normed = ((floats - row_mean) * lax.rsqrt(row_var + norm_epsilon)).astype(jnp.bfloat16)
    qkv_cols = qkv_weight.shape[1]
    heads_dev = qkv_cols // (3 * HD)
    heads_n = lax.axis_size("heads")
    spread = jnp.broadcast_to(normed[None], (heads_n,) + normed.shape)
    block_f = (
        lax.all_to_all(spread, "heads", 0, 0, tiled=False)
        .reshape(heads_n * normed.shape[0], normed.shape[1])
        .astype(jnp.float32)
    )
    attn_in = (block_f * attn_gain + attn_shift).astype(jnp.bfloat16)
    mlp_in = (block_f * mlp_gain + mlp_shift).astype(jnp.bfloat16)
    projected = jnp.concatenate(
        [
            jnp.dot(attn_in, qkv_weight, preferred_element_type=jnp.float32),
            jnp.dot(mlp_in, up_weight, preferred_element_type=jnp.float32),
        ],
        axis=1,
    )
    qkv_part = projected[:, :qkv_cols]
    up_part = projected[:, qkv_cols:]
    all_tokens = projected.shape[0]
    own_rows = all_tokens // lax.axis_size("width")
    row_zero = lax.axis_index("width") * own_rows
    positions = positions_of(segment_ids)
    own_segments = lax.dynamic_slice_in_dim(segment_ids, row_zero, own_rows)
    own_index = row_zero + jnp.arange(own_rows, dtype=jnp.int32)
    score_scale = 1.0 / HD**0.5
    own_positions = lax.dynamic_slice_in_dim(positions, row_zero, own_rows)
    qkv_own, up_own = (
        lax.psum_scatter(qkv_part, "width", scatter_dimension=0, tiled=True),
        lax.psum_scatter(up_part, "width", scatter_dimension=0, tiled=True),
    )
    shaped = (qkv_own + qkv_bias).reshape(qkv_own.shape[0], heads_dev, 3, HD)
    queries = rotary(shaped[:, :, 0, :], own_positions).astype(jnp.bfloat16)
    keys_part = rotary(shaped[:, :, 1, :], own_positions).astype(jnp.bfloat16)
    values_part = shaped[:, :, 2, :].astype(jnp.bfloat16)
    width_cols = heads_dev * HD
    key_cache = keys_part.reshape(-1, width_cols)
    value_cache = values_part.reshape(-1, width_cols)
    run_max = jnp.full((heads_dev, own_rows), -1e30, jnp.float32)
    key_rows = lax.all_gather(key_cache, "width", axis=0, tiled=True)
    value_rows = lax.all_gather(value_cache, "width", axis=0, tiled=True)
    count = key_rows.shape[0]
    key_heads = key_rows.reshape(count, heads_dev, HD)
    value_heads = value_rows.reshape(count, heads_dev, HD)
    scores = (
        jnp.einsum("rhd,nhd->hrn", queries, key_heads, preferred_element_type=jnp.float32)
        * score_scale
    )
    key_index = jnp.arange(count, dtype=jnp.int32)
    allowed = (own_segments[:, None] == segment_ids[None, :]) & (
        key_index[None, :] <= own_index[:, None]
    )
    scores = jnp.where(allowed[None], scores, -1e30)
    new_max = jnp.maximum(run_max, jnp.max(scores, -1))
    weights = jnp.where(allowed[None], jnp.exp(scores - new_max[..., None]), 0.0)
    new_sum = jnp.sum(weights, -1)
    mixed = jnp.einsum(
        "hrn,nhd->hrd",
        weights.astype(jnp.bfloat16),
        value_heads,
        preferred_element_type=jnp.float32,
    )
    attended = (
        (mixed / new_sum[..., None])
        .transpose(1, 0, 2)
        .reshape(own_rows, heads_dev * HD)
        .astype(jnp.bfloat16)
    )
    attn_part = jnp.dot(
        lax.all_gather(attended, "width", axis=0, tiled=True),
        dense_weight,
        preferred_element_type=jnp.float32,
    )
    hidden = jax.nn.gelu(up_own + up_bias, approximate=False).astype(jnp.bfloat16)
    mlp_part = jnp.dot(
        lax.all_gather(hidden, "width", axis=0, tiled=True),
        down_weight,
        preferred_element_type=jnp.float32,
    )
    partial = (attn_part + mlp_part).astype(jnp.bfloat16)
    pieces = partial.reshape(heads_n, partial.shape[0] // heads_n, partial.shape[1])
    summed = jnp.sum(
        lax.all_to_all(pieces, "heads", 0, 0, tiled=False).astype(jnp.float32), 0
    )
    layer_out = (floats + summed + dense_bias + down_bias).astype(jnp.bfloat16)
    return (layer_out, key_cache, value_cache)


def solution(mesh):
    in_specs = (
        P("heads", "width"),
        P(),
        P("width"),
        P("width"),
        P("width"),
        P("width"),
        P("width", "heads"),
        P("heads"),
        P("heads", "width"),
        P("width"),
        P("width", "heads"),
        P("heads"),
        P("heads", "width"),
        P("width"),
    )
    out_specs = (P("heads", "width"), P("width", "heads"), P("width", "heads"))
    return jax.shard_map(
        on_device, mesh=mesh, in_specs=in_specs, out_specs=out_specs, check_vma=False
    )
```

```python
import jax
import jax.numpy as jnp
from jax import lax
from jax.sharding import PartitionSpec as P

HD = 96
ROT = 24
D = 6144


norm_epsilon = 1e-05


def positions_of(segments):
    count = segments.shape[0]
    row_index = jnp.arange(count, dtype=jnp.int32)
    change = jnp.concatenate([jnp.ones((1,), bool), segments[1:] != segments[:-1]])
    first = lax.cummax(jnp.where(change, row_index, 0), axis=0)
    return (row_index - first).astype(jnp.float32)


def rotary(values, positions):
    half_rot = ROT // 2
    inverse = 10000.0 ** (-(jnp.arange(half_rot, dtype=jnp.float32) * 2.0 / ROT))
    angles = positions[:, None] * inverse[None, :]
    cosine = jnp.cos(angles)[:, None, :]
    sine_part = jnp.sin(angles)[:, None, :]
    first_half = values[..., :half_rot]
    second_half = values[..., half_rot:ROT]
    return jnp.concatenate(
        [
            first_half * cosine - second_half * sine_part,
            second_half * cosine + first_half * sine_part,
            values[..., ROT:],
        ],
        axis=-1,
    )


def on_device(
    states,
    segment_ids,
    attn_gain,
    attn_shift,
    mlp_gain,
    mlp_shift,
    qkv_weight,
    qkv_bias,
    dense_weight,
    dense_bias,
    up_weight,
    up_bias,
    down_weight,
    down_bias,
):
    floats = states.astype(jnp.float32)
    row_sums, square_sums = lax.psum((jnp.sum(floats, -1), jnp.sum(floats * floats, -1)), "width")
    row_mean = (row_sums / D)[:, None]
    row_var = (square_sums / D)[:, None] - row_mean * row_mean
    normed = ((floats - row_mean) * lax.rsqrt(row_var + norm_epsilon)).astype(jnp.bfloat16)
    qkv_cols = qkv_weight.shape[1]
    heads_dev = qkv_cols // (3 * HD)
    heads_n = lax.axis_size("heads")
    spread = jnp.broadcast_to(normed[None], (heads_n,) + normed.shape)
    block_f = (
        lax.all_to_all(spread, "heads", 0, 0, tiled=False)
        .reshape(heads_n * normed.shape[0], normed.shape[1])
        .astype(jnp.float32)
    )
    attn_in = (block_f * attn_gain + attn_shift).astype(jnp.bfloat16)
    mlp_in = (block_f * mlp_gain + mlp_shift).astype(jnp.bfloat16)
    projected = jnp.concatenate(
        [
            jnp.dot(attn_in, qkv_weight, preferred_element_type=jnp.float32),
            jnp.dot(mlp_in, up_weight, preferred_element_type=jnp.float32),
        ],
        axis=1,
    )
    qkv_part = projected[:, :qkv_cols]
    up_part = projected[:, qkv_cols:]
    all_tokens = projected.shape[0]
    own_rows = all_tokens // lax.axis_size("width")
    row_zero = lax.axis_index("width") * own_rows
    positions = positions_of(segment_ids)
    own_segments = lax.dynamic_slice_in_dim(segment_ids, row_zero, own_rows)
    own_index = row_zero + jnp.arange(own_rows, dtype=jnp.int32)
    score_scale = 1.0 / HD**0.5
    own_positions = lax.dynamic_slice_in_dim(positions, row_zero, own_rows)
    qkv_own = lax.psum_scatter(
        qkv_part.astype(jnp.bfloat16), "width", scatter_dimension=0, tiled=True
    ).astype(jnp.float32)
    shaped = (qkv_own + qkv_bias).reshape(qkv_own.shape[0], heads_dev, 3, HD)
    queries = rotary(shaped[:, :, 0, :], own_positions).astype(jnp.bfloat16)
    keys_part = rotary(shaped[:, :, 1, :], own_positions).astype(jnp.bfloat16)
    values_part = shaped[:, :, 2, :].astype(jnp.bfloat16)
    width_cols = heads_dev * HD
    key_cache = keys_part.reshape(-1, width_cols)
    value_cache = values_part.reshape(-1, width_cols)
    run_max = jnp.full((heads_dev, own_rows), -1e30, jnp.float32)
    kv_rows = lax.all_gather(
        jnp.concatenate([key_cache, value_cache], axis=1), "width", axis=0, tiled=True
    )
    kv_rows, up_part = lax.optimization_barrier((kv_rows, up_part))
    up_own = lax.psum_scatter(
        up_part.astype(jnp.bfloat16), "width", scatter_dimension=0, tiled=True
    ).astype(jnp.float32)
    key_rows = kv_rows[:, :width_cols]
    value_rows = kv_rows[:, width_cols:]
    count = key_rows.shape[0]
    key_heads = key_rows.reshape(count, heads_dev, HD)
    value_heads = value_rows.reshape(count, heads_dev, HD)
    scores = (
        jnp.einsum("rhd,nhd->hrn", queries, key_heads, preferred_element_type=jnp.float32)
        * score_scale
    )
    key_index = jnp.arange(count, dtype=jnp.int32)
    allowed = (own_segments[:, None] == segment_ids[None, :]) & (
        key_index[None, :] <= own_index[:, None]
    )
    scores = jnp.where(allowed[None], scores, -1e30)
    new_max = jnp.maximum(run_max, jnp.max(scores, -1))
    weights = jnp.where(allowed[None], jnp.exp(scores - new_max[..., None]), 0.0)
    new_sum = jnp.sum(weights, -1)
    mixed = jnp.einsum(
        "hrn,nhd->hrd",
        weights.astype(jnp.bfloat16),
        value_heads,
        preferred_element_type=jnp.float32,
    )
    attended = (
        (mixed / new_sum[..., None])
        .transpose(1, 0, 2)
        .reshape(own_rows, heads_dev * HD)
        .astype(jnp.bfloat16)
    )
    attn_part = jnp.dot(
        lax.all_gather(attended, "width", axis=0, tiled=True),
        dense_weight,
        preferred_element_type=jnp.float32,
    )
    hidden = jax.nn.gelu(up_own + up_bias, approximate=False).astype(jnp.bfloat16)
    mlp_part = jnp.dot(
        lax.all_gather(hidden, "width", axis=0, tiled=True),
        down_weight,
        preferred_element_type=jnp.float32,
    )
    partial = (attn_part + mlp_part).astype(jnp.bfloat16)
    pieces = partial.reshape(heads_n, partial.shape[0] // heads_n, partial.shape[1])
    summed = jnp.sum(
        lax.all_to_all(pieces, "heads", 0, 0, tiled=False).astype(jnp.float32), 0
    )
    layer_out = (floats + summed + dense_bias + down_bias).astype(jnp.bfloat16)
    return (layer_out, key_cache, value_cache)


def solution(mesh):
    in_specs = (
        P("heads", "width"),
        P(),
        P("width"),
        P("width"),
        P("width"),
        P("width"),
        P("width", "heads"),
        P("heads"),
        P("heads", "width"),
        P("width"),
        P("width", "heads"),
        P("heads"),
        P("heads", "width"),
        P("width"),
    )
    out_specs = (P("heads", "width"), P("width", "heads"), P("width", "heads"))
    return jax.shard_map(
        on_device, mesh=mesh, in_specs=in_specs, out_specs=out_specs, check_vma=False
    )
```

```python
import jax
import jax.numpy as jnp
from jax import lax
from jax.sharding import PartitionSpec as P

HD = 96
ROT = 24
D = 6144


norm_epsilon = 1e-05


def positions_of(segments):
    count = segments.shape[0]
    row_index = jnp.arange(count, dtype=jnp.int32)
    change = jnp.concatenate([jnp.ones((1,), bool), segments[1:] != segments[:-1]])
    first = lax.cummax(jnp.where(change, row_index, 0), axis=0)
    return (row_index - first).astype(jnp.float32)


def rotary(values, positions):
    half_rot = ROT // 2
    inverse = 10000.0 ** (-(jnp.arange(half_rot, dtype=jnp.float32) * 2.0 / ROT))
    angles = positions[:, None] * inverse[None, :]
    cosine = jnp.cos(angles)[:, None, :]
    sine_part = jnp.sin(angles)[:, None, :]
    first_half = values[..., :half_rot]
    second_half = values[..., half_rot:ROT]
    return jnp.concatenate(
        [
            first_half * cosine - second_half * sine_part,
            second_half * cosine + first_half * sine_part,
            values[..., ROT:],
        ],
        axis=-1,
    )


HEADS = ("hz", "hy", "hx")
WIDTH = ("wz", "wc")


def gather_heads(block):
    rows, cols = block.shape
    sizes = [lax.axis_size(a) for a in HEADS]
    for axis, size in zip(HEADS, sizes):
        spread = jnp.broadcast_to(block[None], (size,) + block.shape)
        block = lax.all_to_all(spread, axis, 0, 0, tiled=False).reshape(-1, cols)
    block = block.reshape(sizes[2], sizes[1], sizes[0], rows, cols).transpose(2, 1, 0, 3, 4)
    return block.reshape(-1, cols)


def reduce_heads(partial):
    sizes = [lax.axis_size(a) for a in HEADS]
    cols = partial.shape[1]
    rows = partial.shape[0] // (sizes[0] * sizes[1] * sizes[2])
    part = partial.reshape(sizes + [rows, cols]).transpose(2, 0, 1, 3, 4)
    part = lax.all_to_all(part, "hx", 0, 0, tiled=False)
    total = jnp.sum(part.astype(jnp.float32), 0)
    part = total.astype(jnp.bfloat16).transpose(1, 0, 2, 3)
    part = lax.all_to_all(part, "hy", 0, 0, tiled=False)
    total = jnp.sum(part.astype(jnp.float32), 0)
    part = lax.all_to_all(total.astype(jnp.bfloat16), "hz", 0, 0, tiled=False)
    return jnp.sum(part.astype(jnp.float32), 0)


def on_device(
    states,
    segment_ids,
    attn_gain,
    attn_shift,
    mlp_gain,
    mlp_shift,
    qkv_weight,
    qkv_bias,
    dense_weight,
    dense_bias,
    up_weight,
    up_bias,
    down_weight,
    down_bias,
):
    floats = states.astype(jnp.float32)
    stats = lax.psum(jnp.stack([jnp.sum(floats, -1), jnp.sum(floats * floats, -1)]), WIDTH)
    row_mean = (stats[0] / D)[:, None]
    row_var = (stats[1] / D)[:, None] - row_mean * row_mean
    normed = ((floats - row_mean) * lax.rsqrt(row_var + norm_epsilon)).astype(jnp.bfloat16)
    qkv_cols = qkv_weight.shape[1]
    heads_dev = qkv_cols // (3 * HD)
    block_f = gather_heads(normed).astype(jnp.float32)
    attn_in = (block_f * attn_gain + attn_shift).astype(jnp.bfloat16)
    mlp_in = (block_f * mlp_gain + mlp_shift).astype(jnp.bfloat16)
    projected = jnp.concatenate(
        [
            jnp.dot(attn_in, qkv_weight, preferred_element_type=jnp.float32),
            jnp.dot(mlp_in, up_weight, preferred_element_type=jnp.float32),
        ],
        axis=1,
    )
    summed_proj = lax.psum(projected.astype(jnp.bfloat16), WIDTH).astype(jnp.float32)
    all_tokens = projected.shape[0]
    own_rows = all_tokens // lax.axis_size(WIDTH)
    row_zero = lax.axis_index(WIDTH) * own_rows
    positions = positions_of(segment_ids)
    own_segments = lax.dynamic_slice_in_dim(segment_ids, row_zero, own_rows)
    own_index = row_zero + jnp.arange(own_rows, dtype=jnp.int32)
    score_scale = 1.0 / HD**0.5
    own_positions = lax.dynamic_slice_in_dim(positions, row_zero, own_rows)
    shaped = (summed_proj[:, :qkv_cols] + qkv_bias).reshape(all_tokens, heads_dev, 3, HD)
    own_shaped = lax.dynamic_slice_in_dim(shaped, row_zero, own_rows)
    queries = rotary(own_shaped[:, :, 0, :], own_positions).astype(jnp.bfloat16)
    key_heads = rotary(shaped[:, :, 1, :], positions).astype(jnp.bfloat16)
    value_heads = shaped[:, :, 2, :].astype(jnp.bfloat16)
    width_cols = heads_dev * HD
    key_cache = lax.dynamic_slice_in_dim(key_heads, row_zero, own_rows).reshape(-1, width_cols)
    value_cache = lax.dynamic_slice_in_dim(value_heads, row_zero, own_rows).reshape(-1, width_cols)
    run_max = jnp.full((heads_dev, own_rows), -1e30, jnp.float32)
    count = all_tokens
    scores = (
        jnp.einsum("rhd,nhd->hrn", queries, key_heads, preferred_element_type=jnp.float32)
        * score_scale
    )
    key_index = jnp.arange(count, dtype=jnp.int32)
    allowed = (own_segments[:, None] == segment_ids[None, :]) & (
        key_index[None, :] <= own_index[:, None]
    )
    scores = jnp.where(allowed[None], scores, -1e30)
    new_max = jnp.maximum(run_max, jnp.max(scores, -1))
    weights = jnp.where(allowed[None], jnp.exp(scores - new_max[..., None]), 0.0)
    new_sum = jnp.sum(weights, -1)
    mixed = jnp.einsum(
        "hrn,nhd->hrd",
        weights.astype(jnp.bfloat16),
        value_heads,
        preferred_element_type=jnp.float32,
    )
    attended = (
        (mixed / new_sum[..., None])
        .transpose(1, 0, 2)
        .reshape(own_rows, heads_dev * HD)
        .astype(jnp.bfloat16)
    )
    attn_part = jnp.dot(
        lax.all_gather(attended, WIDTH, axis=0, tiled=True),
        dense_weight,
        preferred_element_type=jnp.float32,
    )
    hidden = jax.nn.gelu(summed_proj[:, qkv_cols:] + up_bias, approximate=False).astype(
        jnp.bfloat16
    )
    mlp_part = jnp.dot(hidden, down_weight, preferred_element_type=jnp.float32)
    summed = reduce_heads((attn_part + mlp_part).astype(jnp.bfloat16))
    layer_out = (floats + summed + dense_bias + down_bias).astype(jnp.bfloat16)
    return (layer_out, key_cache, value_cache)


def solution(mesh):
    devices = mesh.devices.reshape(2, 4, 4, 4, 2)
    fine = jax.sharding.Mesh(devices, HEADS + WIDTH)
    in_specs = (
        P(HEADS, WIDTH),
        P(),
        P(WIDTH),
        P(WIDTH),
        P(WIDTH),
        P(WIDTH),
        P(WIDTH, HEADS),
        P(HEADS),
        P(HEADS, WIDTH),
        P(WIDTH),
        P(WIDTH, HEADS),
        P(HEADS),
        P(HEADS, WIDTH),
        P(WIDTH),
    )
    out_specs = (P(HEADS, WIDTH), P(WIDTH, HEADS), P(WIDTH, HEADS))
    return jax.shard_map(
        on_device, mesh=fine, in_specs=in_specs, out_specs=out_specs, check_vma=False
    )
```

```python
import jax
import jax.numpy as jnp
from jax import lax
from jax.sharding import PartitionSpec as P

HD = 96
ROT = 24
D = 6144


norm_epsilon = 1e-05


def positions_of(segments):
    count = segments.shape[0]
    row_index = jnp.arange(count, dtype=jnp.int32)
    change = jnp.concatenate([jnp.ones((1,), bool), segments[1:] != segments[:-1]])
    first = lax.cummax(jnp.where(change, row_index, 0), axis=0)
    return (row_index - first).astype(jnp.float32)


def rotary(values, positions):
    half_rot = ROT // 2
    inverse = 10000.0 ** (-(jnp.arange(half_rot, dtype=jnp.float32) * 2.0 / ROT))
    angles = positions[:, None] * inverse[None, :]
    cosine = jnp.cos(angles)[:, None, :]
    sine_part = jnp.sin(angles)[:, None, :]
    first_half = values[..., :half_rot]
    second_half = values[..., half_rot:ROT]
    return jnp.concatenate(
        [
            first_half * cosine - second_half * sine_part,
            second_half * cosine + first_half * sine_part,
            values[..., ROT:],
        ],
        axis=-1,
    )


HEADS = ("hz", "hy", "hx")
WIDTH = ("wz", "wc")


def gather_heads(block):
    rows, cols = block.shape
    sizes = [lax.axis_size(a) for a in HEADS]
    for axis, size in zip(HEADS, sizes):
        spread = jnp.broadcast_to(block[None], (size,) + block.shape)
        block = lax.all_to_all(spread, axis, 0, 0, tiled=False).reshape(-1, cols)
    block = block.reshape(sizes[2], sizes[1], sizes[0], rows, cols).transpose(2, 1, 0, 3, 4)
    return block.reshape(-1, cols)


def reduce_heads(partial):
    sizes = [lax.axis_size(a) for a in HEADS]
    cols = partial.shape[1]
    rows = partial.shape[0] // (sizes[0] * sizes[1] * sizes[2])
    part = partial.reshape(sizes + [rows, cols]).transpose(2, 0, 1, 3, 4)
    part = lax.all_to_all(part, "hx", 0, 0, tiled=False)
    total = jnp.sum(part.astype(jnp.float32), 0)
    part = total.astype(jnp.bfloat16).transpose(1, 0, 2, 3)
    part = lax.all_to_all(part, "hy", 0, 0, tiled=False)
    total = jnp.sum(part.astype(jnp.float32), 0)
    part = lax.all_to_all(total.astype(jnp.bfloat16), "hz", 0, 0, tiled=False)
    return jnp.sum(part.astype(jnp.float32), 0)


def on_device(
    states,
    segment_ids,
    attn_gain,
    attn_shift,
    mlp_gain,
    mlp_shift,
    qkv_weight,
    qkv_bias,
    dense_weight,
    dense_bias,
    up_weight,
    up_bias,
    down_weight,
    down_bias,
):
    floats = states.astype(jnp.float32)
    stats = lax.psum(jnp.stack([jnp.sum(floats, -1), jnp.sum(floats * floats, -1)]), WIDTH)
    row_mean = (stats[0] / D)[:, None]
    row_var = (stats[1] / D)[:, None] - row_mean * row_mean
    normed = ((floats - row_mean) * lax.rsqrt(row_var + norm_epsilon)).astype(jnp.bfloat16)
    qkv_cols = qkv_weight.shape[1]
    heads_dev = qkv_cols // (3 * HD)
    block_f = gather_heads(normed).astype(jnp.float32)
    attn_in = (block_f * attn_gain + attn_shift).astype(jnp.bfloat16)
    mlp_in = (block_f * mlp_gain + mlp_shift).astype(jnp.bfloat16)
    projected = jnp.concatenate(
        [
            jnp.dot(attn_in, qkv_weight, preferred_element_type=jnp.float32),
            jnp.dot(mlp_in, up_weight, preferred_element_type=jnp.float32),
        ],
        axis=1,
    )
    summed_proj = lax.psum(projected.astype(jnp.bfloat16), WIDTH).astype(jnp.float32)
    all_tokens = projected.shape[0]
    own_rows = all_tokens // lax.axis_size(WIDTH)
    row_zero = lax.axis_index(WIDTH) * own_rows
    positions = positions_of(segment_ids)
    own_segments = lax.dynamic_slice_in_dim(segment_ids, row_zero, own_rows)
    own_index = row_zero + jnp.arange(own_rows, dtype=jnp.int32)
    score_scale = 1.0 / HD**0.5
    own_positions = lax.dynamic_slice_in_dim(positions, row_zero, own_rows)
    shaped = (summed_proj[:, :qkv_cols] + qkv_bias).reshape(all_tokens, heads_dev, 3, HD)
    own_shaped = lax.dynamic_slice_in_dim(shaped, row_zero, own_rows)
    queries = rotary(own_shaped[:, :, 0, :], own_positions).astype(jnp.bfloat16)
    key_heads = rotary(shaped[:, :, 1, :], positions).astype(jnp.bfloat16)
    value_heads = shaped[:, :, 2, :].astype(jnp.bfloat16)
    width_cols = heads_dev * HD
    key_cache = lax.dynamic_slice_in_dim(key_heads, row_zero, own_rows).reshape(-1, width_cols)
    value_cache = lax.dynamic_slice_in_dim(value_heads, row_zero, own_rows).reshape(-1, width_cols)
    run_max = jnp.full((heads_dev, own_rows), -1e30, jnp.float32)
    count = all_tokens
    scores = (
        jnp.einsum("rhd,nhd->hrn", queries, key_heads, preferred_element_type=jnp.float32)
        * score_scale
    )
    key_index = jnp.arange(count, dtype=jnp.int32)
    allowed = (own_segments[:, None] == segment_ids[None, :]) & (
        key_index[None, :] <= own_index[:, None]
    )
    scores = jnp.where(allowed[None], scores, -1e30)
    new_max = jnp.maximum(run_max, jnp.max(scores, -1))
    weights = jnp.where(allowed[None], jnp.exp(scores - new_max[..., None]), 0.0)
    new_sum = jnp.sum(weights, -1)
    mixed = jnp.einsum(
        "hrn,nhd->hrd",
        weights.astype(jnp.bfloat16),
        value_heads,
        preferred_element_type=jnp.float32,
    )
    attended = (
        (mixed / new_sum[..., None])
        .transpose(1, 0, 2)
        .reshape(own_rows, heads_dev * HD)
        .astype(jnp.bfloat16)
    )
    attn_part = jnp.dot(
        lax.all_gather(attended, WIDTH, axis=0, tiled=True),
        dense_weight,
        preferred_element_type=jnp.float32,
    )
    hidden = jax.nn.gelu(summed_proj[:, qkv_cols:] + up_bias, approximate=False).astype(
        jnp.bfloat16
    )
    hidden = lax.optimization_barrier(hidden)
    mlp_part = jnp.dot(hidden, down_weight, preferred_element_type=jnp.float32)
    summed = reduce_heads((attn_part + mlp_part).astype(jnp.bfloat16))
    layer_out = (floats + summed + dense_bias + down_bias).astype(jnp.bfloat16)
    return (layer_out, key_cache, value_cache)


def solution(mesh):
    devices = mesh.devices.reshape(2, 4, 4, 4, 2)
    fine = jax.sharding.Mesh(devices, HEADS + WIDTH)
    in_specs = (
        P(HEADS, WIDTH),
        P(),
        P(WIDTH),
        P(WIDTH),
        P(WIDTH),
        P(WIDTH),
        P(WIDTH, HEADS),
        P(HEADS),
        P(HEADS, WIDTH),
        P(WIDTH),
        P(WIDTH, HEADS),
        P(HEADS),
        P(HEADS, WIDTH),
        P(WIDTH),
    )
    out_specs = (P(HEADS, WIDTH), P(WIDTH, HEADS), P(WIDTH, HEADS))
    return jax.shard_map(
        on_device, mesh=fine, in_specs=in_specs, out_specs=out_specs, check_vma=False
    )
```

```python
import jax
import jax.numpy as jnp
from jax import lax
from jax.sharding import PartitionSpec as P

HD = 96
ROT = 24
D = 6144


norm_epsilon = 1e-05


def positions_of(segments):
    count = segments.shape[0]
    row_index = jnp.arange(count, dtype=jnp.int32)
    change = jnp.concatenate([jnp.ones((1,), bool), segments[1:] != segments[:-1]])
    first = lax.cummax(jnp.where(change, row_index, 0), axis=0)
    return (row_index - first).astype(jnp.float32)


def rotary(values, positions):
    half_rot = ROT // 2
    inverse = 10000.0 ** (-(jnp.arange(half_rot, dtype=jnp.float32) * 2.0 / ROT))
    angles = positions[:, None] * inverse[None, :]
    cosine = jnp.cos(angles)[:, None, :]
    sine_part = jnp.sin(angles)[:, None, :]
    first_half = values[..., :half_rot]
    second_half = values[..., half_rot:ROT]
    return jnp.concatenate(
        [
            first_half * cosine - second_half * sine_part,
            second_half * cosine + first_half * sine_part,
            values[..., ROT:],
        ],
        axis=-1,
    )


HEADS = ("hz", "hy", "hx")
WIDTH = ("wz", "wc")


def gather_heads(block):
    rows, cols = block.shape
    nz, ny, nx = [lax.axis_size(a) for a in HEADS]
    spread = jnp.broadcast_to(block[None], (nz,) + block.shape)
    block = lax.all_to_all(spread, "hz", 0, 0, tiled=False).reshape(-1, cols)
    spread = jnp.broadcast_to(block[None], (ny * nx,) + block.shape)
    block = lax.all_to_all(spread, ("hy", "hx"), 0, 0, tiled=False)
    block = block.reshape(ny, nx, nz, rows, cols).transpose(2, 0, 1, 3, 4)
    return block.reshape(-1, cols)


def reduce_heads(partial):
    nz, ny, nx = [lax.axis_size(a) for a in HEADS]
    cols = partial.shape[1]
    rows = partial.shape[0] // (nz * ny * nx)
    part = partial.reshape(nz, ny * nx, rows, cols).transpose(1, 0, 2, 3)
    part = lax.all_to_all(part, ("hy", "hx"), 0, 0, tiled=False)
    total = jnp.sum(part.astype(jnp.float32), 0)
    part = lax.all_to_all(total.astype(jnp.bfloat16), "hz", 0, 0, tiled=False)
    return jnp.sum(part.astype(jnp.float32), 0)


def on_device(
    states,
    segment_ids,
    attn_gain,
    attn_shift,
    mlp_gain,
    mlp_shift,
    qkv_weight,
    qkv_bias,
    dense_weight,
    dense_bias,
    up_weight,
    up_bias,
    down_weight,
    down_bias,
):
    floats = states.astype(jnp.float32)
    stats = lax.psum(jnp.stack([jnp.sum(floats, -1), jnp.sum(floats * floats, -1)]), WIDTH)
    row_mean = (stats[0] / D)[:, None]
    row_var = (stats[1] / D)[:, None] - row_mean * row_mean
    normed = ((floats - row_mean) * lax.rsqrt(row_var + norm_epsilon)).astype(jnp.bfloat16)
    qkv_cols = qkv_weight.shape[1]
    heads_dev = qkv_cols // (3 * HD)
    block_f = gather_heads(normed).astype(jnp.float32)
    attn_in = (block_f * attn_gain + attn_shift).astype(jnp.bfloat16)
    mlp_in = (block_f * mlp_gain + mlp_shift).astype(jnp.bfloat16)
    projected = jnp.concatenate(
        [
            jnp.dot(attn_in, qkv_weight, preferred_element_type=jnp.float32),
            jnp.dot(mlp_in, up_weight, preferred_element_type=jnp.float32),
        ],
        axis=1,
    )
    summed_proj = lax.psum(projected.astype(jnp.bfloat16), WIDTH).astype(jnp.float32)
    all_tokens = projected.shape[0]
    own_rows = all_tokens // lax.axis_size(WIDTH)
    row_zero = lax.axis_index(WIDTH) * own_rows
    positions = positions_of(segment_ids)
    own_segments = lax.dynamic_slice_in_dim(segment_ids, row_zero, own_rows)
    own_index = row_zero + jnp.arange(own_rows, dtype=jnp.int32)
    score_scale = 1.0 / HD**0.5
    own_positions = lax.dynamic_slice_in_dim(positions, row_zero, own_rows)
    shaped = (summed_proj[:, :qkv_cols] + qkv_bias).reshape(all_tokens, heads_dev, 3, HD)
    own_shaped = lax.dynamic_slice_in_dim(shaped, row_zero, own_rows)
    queries = rotary(own_shaped[:, :, 0, :], own_positions).astype(jnp.bfloat16)
    key_heads = rotary(shaped[:, :, 1, :], positions).astype(jnp.bfloat16)
    value_heads = shaped[:, :, 2, :].astype(jnp.bfloat16)
    width_cols = heads_dev * HD
    key_cache = lax.dynamic_slice_in_dim(key_heads, row_zero, own_rows).reshape(-1, width_cols)
    value_cache = lax.dynamic_slice_in_dim(value_heads, row_zero, own_rows).reshape(-1, width_cols)
    run_max = jnp.full((heads_dev, own_rows), -1e30, jnp.float32)
    count = all_tokens
    scores = (
        jnp.einsum("rhd,nhd->hrn", queries, key_heads, preferred_element_type=jnp.float32)
        * score_scale
    )
    key_index = jnp.arange(count, dtype=jnp.int32)
    allowed = (own_segments[:, None] == segment_ids[None, :]) & (
        key_index[None, :] <= own_index[:, None]
    )
    scores = jnp.where(allowed[None], scores, -1e30)
    new_max = jnp.maximum(run_max, jnp.max(scores, -1))
    weights = jnp.where(allowed[None], jnp.exp(scores - new_max[..., None]), 0.0)
    new_sum = jnp.sum(weights, -1)
    mixed = jnp.einsum(
        "hrn,nhd->hrd",
        weights.astype(jnp.bfloat16),
        value_heads,
        preferred_element_type=jnp.float32,
    )
    attended = (
        (mixed / new_sum[..., None])
        .transpose(1, 0, 2)
        .reshape(own_rows, heads_dev * HD)
        .astype(jnp.bfloat16)
    )
    attn_part = jnp.dot(
        lax.all_gather(attended, WIDTH, axis=0, tiled=True),
        dense_weight,
        preferred_element_type=jnp.float32,
    )
    hidden = jax.nn.gelu(summed_proj[:, qkv_cols:] + up_bias, approximate=False).astype(
        jnp.bfloat16
    )
    hidden = lax.optimization_barrier(hidden)
    mlp_part = jnp.dot(hidden, down_weight, preferred_element_type=jnp.float32)
    summed = reduce_heads((attn_part + mlp_part).astype(jnp.bfloat16))
    layer_out = (floats + summed + dense_bias + down_bias).astype(jnp.bfloat16)
    return (layer_out, key_cache, value_cache)


def solution(mesh):
    devices = mesh.devices.reshape(2, 4, 4, 4, 2)
    fine = jax.sharding.Mesh(devices, HEADS + WIDTH)
    in_specs = (
        P(HEADS, WIDTH),
        P(),
        P(WIDTH),
        P(WIDTH),
        P(WIDTH),
        P(WIDTH),
        P(WIDTH, HEADS),
        P(HEADS),
        P(HEADS, WIDTH),
        P(WIDTH),
        P(WIDTH, HEADS),
        P(HEADS),
        P(HEADS, WIDTH),
        P(WIDTH),
    )
    out_specs = (P(HEADS, WIDTH), P(WIDTH, HEADS), P(WIDTH, HEADS))
    return jax.shard_map(
        on_device, mesh=fine, in_specs=in_specs, out_specs=out_specs, check_vma=False
    )
```

```python
import jax
import jax.numpy as jnp
from jax import lax
from jax.sharding import PartitionSpec as P

HD = 96
ROT = 24
D = 6144


norm_epsilon = 1e-05


def positions_of(segments):
    count = segments.shape[0]
    row_index = jnp.arange(count, dtype=jnp.int32)
    change = jnp.concatenate([jnp.ones((1,), bool), segments[1:] != segments[:-1]])
    first = lax.cummax(jnp.where(change, row_index, 0), axis=0)
    return (row_index - first).astype(jnp.float32)


def rotary(values, positions):
    half_rot = ROT // 2
    inverse = 10000.0 ** (-(jnp.arange(half_rot, dtype=jnp.float32) * 2.0 / ROT))
    angles = positions[:, None] * inverse[None, :]
    cosine = jnp.cos(angles)[:, None, :]
    sine_part = jnp.sin(angles)[:, None, :]
    first_half = values[..., :half_rot]
    second_half = values[..., half_rot:ROT]
    return jnp.concatenate(
        [
            first_half * cosine - second_half * sine_part,
            second_half * cosine + first_half * sine_part,
            values[..., ROT:],
        ],
        axis=-1,
    )


HEADS = ("hz", "hy", "hx")
WIDTH = ("wz", "wc")


def gather_heads(block):
    rows, cols = block.shape
    nz, ny, nx = [lax.axis_size(a) for a in HEADS]
    spread = jnp.broadcast_to(block[None], (nz,) + block.shape)
    block = lax.all_to_all(spread, "hz", 0, 0, tiled=False).reshape(-1, cols)
    spread = jnp.broadcast_to(block[None], (ny * nx,) + block.shape)
    block = lax.all_to_all(spread, ("hy", "hx"), 0, 0, tiled=False)
    block = block.reshape(ny, nx, nz, rows, cols).transpose(2, 0, 1, 3, 4)
    return block.reshape(-1, cols)


def reduce_heads(partial):
    nz, ny, nx = [lax.axis_size(a) for a in HEADS]
    cols = partial.shape[1]
    rows = partial.shape[0] // (nz * ny * nx)
    part = partial.reshape(nz, ny * nx, rows, cols).transpose(1, 0, 2, 3)
    part = lax.all_to_all(part, ("hy", "hx"), 0, 0, tiled=False)
    total = jnp.sum(part.astype(jnp.float32), 0)
    part = lax.all_to_all(total.astype(jnp.bfloat16), "hz", 0, 0, tiled=False)
    return jnp.sum(part.astype(jnp.float32), 0)


def on_device(
    states,
    segment_ids,
    attn_gain,
    attn_shift,
    mlp_gain,
    mlp_shift,
    qkv_weight,
    qkv_bias,
    dense_weight,
    dense_bias,
    up_weight,
    up_bias,
    down_weight,
    down_bias,
):
    floats = states.astype(jnp.float32)
    stats = lax.psum(jnp.stack([jnp.sum(floats, -1), jnp.sum(floats * floats, -1)]), WIDTH)
    row_mean = (stats[0] / D)[:, None]
    row_var = (stats[1] / D)[:, None] - row_mean * row_mean
    normed = ((floats - row_mean) * lax.rsqrt(row_var + norm_epsilon)).astype(jnp.bfloat16)
    qkv_cols = qkv_weight.shape[1]
    heads_dev = qkv_cols // (3 * HD)
    block_f = gather_heads(normed).astype(jnp.float32)
    attn_in = (block_f * attn_gain + attn_shift).astype(jnp.bfloat16)
    mlp_in = (block_f * mlp_gain + mlp_shift).astype(jnp.bfloat16)
    projected = jnp.concatenate(
        [
            jnp.dot(attn_in, qkv_weight, preferred_element_type=jnp.float32),
            jnp.dot(mlp_in, up_weight, preferred_element_type=jnp.float32),
        ],
        axis=1,
    )
    summed_proj = lax.psum(projected.astype(jnp.bfloat16), WIDTH).astype(jnp.float32)
    all_tokens = projected.shape[0]
    own_rows = all_tokens // lax.axis_size(WIDTH)
    row_zero = lax.axis_index(WIDTH) * own_rows
    positions = positions_of(segment_ids)
    own_segments = lax.dynamic_slice_in_dim(segment_ids, row_zero, own_rows)
    own_index = row_zero + jnp.arange(own_rows, dtype=jnp.int32)
    score_scale = 1.0 / HD**0.5
    own_positions = lax.dynamic_slice_in_dim(positions, row_zero, own_rows)
    shaped = (summed_proj[:, :qkv_cols] + qkv_bias).reshape(all_tokens, heads_dev, 3, HD)
    own_shaped = lax.dynamic_slice_in_dim(shaped, row_zero, own_rows)
    queries = rotary(own_shaped[:, :, 0, :], own_positions).astype(jnp.bfloat16)
    key_heads = rotary(shaped[:, :, 1, :], positions).astype(jnp.bfloat16)
    value_heads = shaped[:, :, 2, :].astype(jnp.bfloat16)
    width_cols = heads_dev * HD
    key_cache = lax.dynamic_slice_in_dim(key_heads, row_zero, own_rows).reshape(-1, width_cols)
    value_cache = lax.dynamic_slice_in_dim(value_heads, row_zero, own_rows).reshape(-1, width_cols)
    run_max = jnp.full((heads_dev, own_rows), -1e30, jnp.float32)
    count = all_tokens
    scores = (
        jnp.einsum("rhd,nhd->hrn", queries, key_heads, preferred_element_type=jnp.float32)
        * score_scale
    )
    key_index = jnp.arange(count, dtype=jnp.int32)
    allowed = (own_segments[:, None] == segment_ids[None, :]) & (
        key_index[None, :] <= own_index[:, None]
    )
    scores = jnp.where(allowed[None], scores, -1e30)
    new_max = jnp.maximum(run_max, jnp.max(scores, -1))
    weights = jnp.where(allowed[None], jnp.exp(scores - new_max[..., None]), 0.0)
    new_sum = jnp.sum(weights, -1)
    mixed = jnp.einsum(
        "hrn,nhd->hrd",
        weights.astype(jnp.bfloat16),
        value_heads,
        preferred_element_type=jnp.float32,
    )
    attended = (
        (mixed / new_sum[..., None])
        .transpose(1, 0, 2)
        .reshape(own_rows, heads_dev * HD)
        .astype(jnp.bfloat16)
    )
    width_n = lax.axis_size(WIDTH)
    shifted = [attended] + [
        lax.ppermute(attended, WIDTH, [(i, (i + k) % width_n) for i in range(width_n)])
        for k in range(1, width_n)
    ]
    sources = (lax.axis_index(WIDTH) - jnp.arange(width_n)) % width_n
    gathered = jnp.take(jnp.stack(shifted), sources, axis=0).reshape(-1, attended.shape[1])
    hidden = jax.nn.gelu(summed_proj[:, qkv_cols:] + up_bias, approximate=False).astype(
        jnp.bfloat16
    )
    hidden = lax.optimization_barrier(hidden)
    mlp_part = jnp.dot(hidden, down_weight, preferred_element_type=jnp.float32)
    attn_part = jnp.dot(gathered, dense_weight, preferred_element_type=jnp.float32)
    summed = reduce_heads((attn_part + mlp_part).astype(jnp.bfloat16))
    layer_out = (floats + summed + dense_bias + down_bias).astype(jnp.bfloat16)
    return (layer_out, key_cache, value_cache)


def solution(mesh):
    devices = mesh.devices.reshape(2, 4, 4, 4, 2)
    fine = jax.sharding.Mesh(devices, HEADS + WIDTH)
    in_specs = (
        P(HEADS, WIDTH),
        P(),
        P(WIDTH),
        P(WIDTH),
        P(WIDTH),
        P(WIDTH),
        P(WIDTH, HEADS),
        P(HEADS),
        P(HEADS, WIDTH),
        P(WIDTH),
        P(WIDTH, HEADS),
        P(HEADS),
        P(HEADS, WIDTH),
        P(WIDTH),
    )
    out_specs = (P(HEADS, WIDTH), P(WIDTH, HEADS), P(WIDTH, HEADS))
    return jax.shard_map(
        on_device, mesh=fine, in_specs=in_specs, out_specs=out_specs, check_vma=False
    )
```

```python
import jax
import jax.numpy as jnp
from jax import lax
from jax.sharding import PartitionSpec as P

HD = 96
ROT = 24
D = 6144


norm_epsilon = 1e-05


def positions_of(segments):
    count = segments.shape[0]
    row_index = jnp.arange(count, dtype=jnp.int32)
    change = jnp.concatenate([jnp.ones((1,), bool), segments[1:] != segments[:-1]])
    first = lax.cummax(jnp.where(change, row_index, 0), axis=0)
    return (row_index - first).astype(jnp.float32)


def rotary(values, positions):
    half_rot = ROT // 2
    inverse = 10000.0 ** (-(jnp.arange(half_rot, dtype=jnp.float32) * 2.0 / ROT))
    angles = positions[:, None] * inverse[None, :]
    cosine = jnp.cos(angles)[:, None, :]
    sine_part = jnp.sin(angles)[:, None, :]
    first_half = values[..., :half_rot]
    second_half = values[..., half_rot:ROT]
    return jnp.concatenate(
        [
            first_half * cosine - second_half * sine_part,
            second_half * cosine + first_half * sine_part,
            values[..., ROT:],
        ],
        axis=-1,
    )


HEADS = ("hz", "hy", "hx")
WIDTH = ("wz", "wc")


def gather_heads(block):
    rows, cols = block.shape
    ny, nx = lax.axis_size("hy"), lax.axis_size("hx")
    spread = jnp.broadcast_to(block[None], (ny * nx,) + block.shape)
    block = lax.all_to_all(spread, ("hy", "hx"), 0, 0, tiled=False)
    nz = lax.axis_size("hz")
    block = block.reshape(ny, nx, nz, rows // nz, cols).transpose(2, 0, 1, 3, 4)
    return block.reshape(-1, cols)


def reduce_heads(partial):
    nz, ny, nx = [lax.axis_size(a) for a in HEADS]
    cols = partial.shape[1]
    rows = partial.shape[0] // (nz * ny * nx)
    part = partial.reshape(nz, ny * nx, rows, cols).transpose(1, 0, 2, 3)
    part = lax.all_to_all(part, ("hy", "hx"), 0, 0, tiled=False)
    total = jnp.sum(part.astype(jnp.float32), 0)
    part = lax.all_to_all(total.astype(jnp.bfloat16), "hz", 0, 0, tiled=False)
    return jnp.sum(part.astype(jnp.float32), 0)


def on_device(
    states,
    segment_ids,
    attn_gain,
    attn_shift,
    mlp_gain,
    mlp_shift,
    qkv_weight,
    qkv_bias,
    dense_weight,
    dense_bias,
    up_weight,
    up_bias,
    down_weight,
    down_bias,
):
    floats = states.astype(jnp.float32)
    nz = lax.axis_size("hz")
    z = lax.axis_index("hz")
    swaps = [lax.ppermute(states, "hz", [(i, (i + k) % nz) for i in range(nz)]) for k in range(1, nz)]
    local = jnp.stack([jnp.sum(floats, -1), jnp.sum(floats * floats, -1)])
    every = lax.all_gather(local, ("hz",) + WIDTH, axis=0, tiled=False)
    stats = jnp.sum(every.reshape(nz, -1, 2, local.shape[1]), 1)
    pair = jnp.stack([states] + swaps)
    by_z = jnp.take(pair, (z - jnp.arange(nz)) % nz, axis=0).astype(jnp.float32)
    row_mean = (stats[:, 0] / D)[..., None]
    row_var = (stats[:, 1] / D)[..., None] - row_mean * row_mean
    normed = ((by_z - row_mean) * lax.rsqrt(row_var + norm_epsilon)).astype(jnp.bfloat16)
    qkv_cols = qkv_weight.shape[1]
    heads_dev = qkv_cols // (3 * HD)
    block_f = gather_heads(normed.reshape(-1, normed.shape[2])).astype(jnp.float32)
    attn_in = (block_f * attn_gain + attn_shift).astype(jnp.bfloat16)
    mlp_in = (block_f * mlp_gain + mlp_shift).astype(jnp.bfloat16)
    projected = jnp.concatenate(
        [
            jnp.dot(attn_in, qkv_weight, preferred_element_type=jnp.float32),
            jnp.dot(mlp_in, up_weight, preferred_element_type=jnp.float32),
        ],
        axis=1,
    )
    summed_proj = lax.psum(projected.astype(jnp.bfloat16), WIDTH).astype(jnp.float32)
    all_tokens = projected.shape[0]
    own_rows = all_tokens // lax.axis_size(WIDTH)
    row_zero = lax.axis_index(WIDTH) * own_rows
    positions = positions_of(segment_ids)
    own_segments = lax.dynamic_slice_in_dim(segment_ids, row_zero, own_rows)
    own_index = row_zero + jnp.arange(own_rows, dtype=jnp.int32)
    score_scale = 1.0 / HD**0.5
    own_positions = lax.dynamic_slice_in_dim(positions, row_zero, own_rows)
    shaped = (summed_proj[:, :qkv_cols] + qkv_bias).reshape(all_tokens, heads_dev, 3, HD)
    own_shaped = lax.dynamic_slice_in_dim(shaped, row_zero, own_rows)
    queries = rotary(own_shaped[:, :, 0, :], own_positions).astype(jnp.bfloat16)
    key_heads = rotary(shaped[:, :, 1, :], positions).astype(jnp.bfloat16)
    value_heads = shaped[:, :, 2, :].astype(jnp.bfloat16)
    width_cols = heads_dev * HD
    key_cache = lax.dynamic_slice_in_dim(key_heads, row_zero, own_rows).reshape(-1, width_cols)
    value_cache = lax.dynamic_slice_in_dim(value_heads, row_zero, own_rows).reshape(-1, width_cols)
    run_max = jnp.full((heads_dev, own_rows), -1e30, jnp.float32)
    count = all_tokens
    scores = (
        jnp.einsum("rhd,nhd->hrn", queries, key_heads, preferred_element_type=jnp.float32)
        * score_scale
    )
    key_index = jnp.arange(count, dtype=jnp.int32)
    allowed = (own_segments[:, None] == segment_ids[None, :]) & (
        key_index[None, :] <= own_index[:, None]
    )
    scores = jnp.where(allowed[None], scores, -1e30)
    new_max = jnp.maximum(run_max, jnp.max(scores, -1))
    weights = jnp.where(allowed[None], jnp.exp(scores - new_max[..., None]), 0.0)
    new_sum = jnp.sum(weights, -1)
    mixed = jnp.einsum(
        "hrn,nhd->hrd",
        weights.astype(jnp.bfloat16),
        value_heads,
        preferred_element_type=jnp.float32,
    )
    attended = (
        (mixed / new_sum[..., None])
        .transpose(1, 0, 2)
        .reshape(own_rows, heads_dev * HD)
        .astype(jnp.bfloat16)
    )
    attn_part = jnp.dot(
        lax.all_gather(attended, WIDTH, axis=0, tiled=True),
        dense_weight,
        preferred_element_type=jnp.float32,
    )
    hidden = jax.nn.gelu(summed_proj[:, qkv_cols:] + up_bias, approximate=False).astype(
        jnp.bfloat16
    )
    hidden = lax.optimization_barrier(hidden)
    mlp_part = jnp.dot(hidden, down_weight, preferred_element_type=jnp.float32)
    summed = reduce_heads((attn_part + mlp_part).astype(jnp.bfloat16))
    layer_out = (floats + summed + dense_bias + down_bias).astype(jnp.bfloat16)
    return (layer_out, key_cache, value_cache)


def solution(mesh):
    devices = mesh.devices.reshape(2, 4, 4, 4, 2)
    fine = jax.sharding.Mesh(devices, HEADS + WIDTH)
    in_specs = (
        P(HEADS, WIDTH),
        P(),
        P(WIDTH),
        P(WIDTH),
        P(WIDTH),
        P(WIDTH),
        P(WIDTH, HEADS),
        P(HEADS),
        P(HEADS, WIDTH),
        P(WIDTH),
        P(WIDTH, HEADS),
        P(HEADS),
        P(HEADS, WIDTH),
        P(WIDTH),
    )
    out_specs = (P(HEADS, WIDTH), P(WIDTH, HEADS), P(WIDTH, HEADS))
    return jax.shard_map(
        on_device, mesh=fine, in_specs=in_specs, out_specs=out_specs, check_vma=False
    )
```

```python
import jax
import jax.numpy as jnp
from jax import lax
from jax.sharding import PartitionSpec as P

HD = 96
ROT = 24
D = 6144


norm_epsilon = 1e-05


def positions_of(segments):
    count = segments.shape[0]
    row_index = jnp.arange(count, dtype=jnp.int32)
    change = jnp.concatenate([jnp.ones((1,), bool), segments[1:] != segments[:-1]])
    first = lax.cummax(jnp.where(change, row_index, 0), axis=0)
    return (row_index - first).astype(jnp.float32)


def rotary(values, positions):
    half_rot = ROT // 2
    inverse = 10000.0 ** (-(jnp.arange(half_rot, dtype=jnp.float32) * 2.0 / ROT))
    angles = positions[:, None] * inverse[None, :]
    cosine = jnp.cos(angles)[:, None, :]
    sine_part = jnp.sin(angles)[:, None, :]
    first_half = values[..., :half_rot]
    second_half = values[..., half_rot:ROT]
    return jnp.concatenate(
        [
            first_half * cosine - second_half * sine_part,
            second_half * cosine + first_half * sine_part,
            values[..., ROT:],
        ],
        axis=-1,
    )


HEADS = ("hz", "hy", "hx")
WIDTH = ("wz", "wc")


def gather_heads(block):
    rows, cols = block.shape
    ny, nx = lax.axis_size("hy"), lax.axis_size("hx")
    spread = jnp.broadcast_to(block[None], (ny * nx,) + block.shape)
    block = lax.all_to_all(spread, ("hy", "hx"), 0, 0, tiled=False)
    nz = lax.axis_size("hz")
    block = block.reshape(ny, nx, nz, rows // nz, cols).transpose(2, 0, 1, 3, 4)
    return block.reshape(-1, cols)


def reduce_heads(partial):
    nz, ny, nx = [lax.axis_size(a) for a in HEADS]
    cols = partial.shape[1]
    rows = partial.shape[0] // (nz * ny * nx)
    part = partial.reshape(nz, ny * nx, rows, cols).transpose(1, 0, 2, 3)
    part = lax.all_to_all(part, ("hy", "hx"), 0, 0, tiled=False)
    total = jnp.sum(part.astype(jnp.float32), 0)
    part = lax.all_to_all(total.astype(jnp.bfloat16), "hz", 0, 0, tiled=False)
    return jnp.sum(part.astype(jnp.float32), 0)


def on_device(
    states,
    segment_ids,
    attn_gain,
    attn_shift,
    mlp_gain,
    mlp_shift,
    qkv_weight,
    qkv_bias,
    dense_weight,
    dense_bias,
    up_weight,
    up_bias,
    down_weight,
    down_bias,
):
    floats = states.astype(jnp.float32)
    nz = lax.axis_size("hz")
    z = lax.axis_index("hz")
    swaps = [lax.ppermute(states, "hz", [(i, (i + k) % nz) for i in range(nz)]) for k in range(1, nz)]
    local = jnp.stack([jnp.sum(floats, -1), jnp.sum(floats * floats, -1)])
    every = lax.all_gather(local, ("hz",) + WIDTH, axis=0, tiled=False)
    stats = jnp.sum(every.reshape(nz, -1, 2, local.shape[1]), 1)
    pair = jnp.stack([states] + swaps)
    by_z = jnp.take(pair, (z - jnp.arange(nz)) % nz, axis=0).astype(jnp.float32)
    row_mean = (stats[:, 0] / D)[..., None]
    row_var = (stats[:, 1] / D)[..., None] - row_mean * row_mean
    normed = ((by_z - row_mean) * lax.rsqrt(row_var + norm_epsilon)).astype(jnp.bfloat16)
    qkv_cols = qkv_weight.shape[1]
    heads_dev = qkv_cols // (3 * HD)
    block_f = gather_heads(normed.reshape(-1, normed.shape[2])).astype(jnp.float32)
    attn_in = (block_f * attn_gain + attn_shift).astype(jnp.bfloat16)
    mlp_in = (block_f * mlp_gain + mlp_shift).astype(jnp.bfloat16)
    projected = jnp.concatenate(
        [
            jnp.dot(attn_in, qkv_weight, preferred_element_type=jnp.float32),
            jnp.dot(mlp_in, up_weight, preferred_element_type=jnp.float32),
        ],
        axis=1,
    )
    summed_proj = lax.psum(projected.astype(jnp.bfloat16), WIDTH)
    all_tokens = projected.shape[0]
    own_rows = all_tokens // lax.axis_size(WIDTH)
    row_zero = lax.axis_index(WIDTH) * own_rows
    positions = positions_of(segment_ids)
    own_segments = lax.dynamic_slice_in_dim(segment_ids, row_zero, own_rows)
    own_index = row_zero + jnp.arange(own_rows, dtype=jnp.int32)
    score_scale = 1.0 / HD**0.5
    own_positions = lax.dynamic_slice_in_dim(positions, row_zero, own_rows)
    shaped = (summed_proj[:, :qkv_cols].astype(jnp.float32) + qkv_bias).reshape(all_tokens, heads_dev, 3, HD)
    own_shaped = lax.dynamic_slice_in_dim(shaped, row_zero, own_rows)
    queries = rotary(own_shaped[:, :, 0, :], own_positions).astype(jnp.bfloat16)
    key_heads = rotary(shaped[:, :, 1, :], positions).astype(jnp.bfloat16)
    value_heads = shaped[:, :, 2, :].astype(jnp.bfloat16)
    width_cols = heads_dev * HD
    key_cache = lax.dynamic_slice_in_dim(key_heads, row_zero, own_rows).reshape(-1, width_cols)
    value_cache = lax.dynamic_slice_in_dim(value_heads, row_zero, own_rows).reshape(-1, width_cols)
    run_max = jnp.full((heads_dev, own_rows), -1e30, jnp.float32)
    count = all_tokens
    scores = (
        jnp.einsum("rhd,nhd->hrn", queries, key_heads, preferred_element_type=jnp.float32)
        * score_scale
    )
    key_index = jnp.arange(count, dtype=jnp.int32)
    allowed = (own_segments[:, None] == segment_ids[None, :]) & (
        key_index[None, :] <= own_index[:, None]
    )
    scores = jnp.where(allowed[None], scores, -1e30)
    new_max = jnp.maximum(run_max, jnp.max(scores, -1))
    weights = jnp.where(allowed[None], jnp.exp(scores - new_max[..., None]), 0.0)
    new_sum = jnp.sum(weights, -1)
    mixed = jnp.einsum(
        "hrn,nhd->hrd",
        weights.astype(jnp.bfloat16),
        value_heads,
        preferred_element_type=jnp.float32,
    )
    attended = (
        (mixed / new_sum[..., None])
        .transpose(1, 0, 2)
        .reshape(own_rows, heads_dev * HD)
        .astype(jnp.bfloat16)
    )
    attn_part = jnp.dot(
        lax.all_gather(attended, WIDTH, axis=0, tiled=True),
        dense_weight,
        preferred_element_type=jnp.float32,
    )
    hidden = jax.nn.gelu(summed_proj[:, qkv_cols:].astype(jnp.float32) + up_bias, approximate=False).astype(
        jnp.bfloat16
    )
    hidden = lax.optimization_barrier(hidden)
    mlp_part = jnp.dot(hidden, down_weight, preferred_element_type=jnp.float32)
    summed = reduce_heads((attn_part + mlp_part).astype(jnp.bfloat16))
    layer_out = (floats + summed + dense_bias + down_bias).astype(jnp.bfloat16)
    return (layer_out, key_cache, value_cache)


def solution(mesh):
    devices = mesh.devices.reshape(2, 4, 4, 4, 2)
    fine = jax.sharding.Mesh(devices, HEADS + WIDTH)
    in_specs = (
        P(HEADS, WIDTH),
        P(),
        P(WIDTH),
        P(WIDTH),
        P(WIDTH),
        P(WIDTH),
        P(WIDTH, HEADS),
        P(HEADS),
        P(HEADS, WIDTH),
        P(WIDTH),
        P(WIDTH, HEADS),
        P(HEADS),
        P(HEADS, WIDTH),
        P(WIDTH),
    )
    out_specs = (P(HEADS, WIDTH), P(WIDTH, HEADS), P(WIDTH, HEADS))
    return jax.shard_map(
        on_device, mesh=fine, in_specs=in_specs, out_specs=out_specs, check_vma=False
    )
```

```python
import jax
import jax.numpy as jnp
from jax import lax
from jax.sharding import PartitionSpec as P

HD = 96
ROT = 24
D = 6144


norm_epsilon = 1e-05


def positions_of(segments):
    count = segments.shape[0]
    row_index = jnp.arange(count, dtype=jnp.int32)
    change = jnp.concatenate([jnp.ones((1,), bool), segments[1:] != segments[:-1]])
    first = lax.cummax(jnp.where(change, row_index, 0), axis=0)
    return (row_index - first).astype(jnp.float32)


def rotary(values, positions):
    half_rot = ROT // 2
    inverse = 10000.0 ** (-(jnp.arange(half_rot, dtype=jnp.float32) * 2.0 / ROT))
    angles = positions[:, None] * inverse[None, :]
    cosine = jnp.cos(angles)[:, None, :]
    sine_part = jnp.sin(angles)[:, None, :]
    first_half = values[..., :half_rot]
    second_half = values[..., half_rot:ROT]
    return jnp.concatenate(
        [
            first_half * cosine - second_half * sine_part,
            second_half * cosine + first_half * sine_part,
            values[..., ROT:],
        ],
        axis=-1,
    )


HEADS = ("hz", "hy", "hx")
WIDTH = ("wz", "wc")


def gather_heads(block):
    rows, cols = block.shape
    ny, nx = lax.axis_size("hy"), lax.axis_size("hx")
    spread = jnp.broadcast_to(block[None], (ny * nx,) + block.shape)
    block = lax.all_to_all(spread, ("hy", "hx"), 0, 0, tiled=False)
    nz = lax.axis_size("hz")
    block = block.reshape(ny, nx, nz, rows // nz, cols).transpose(2, 0, 1, 3, 4)
    return block.reshape(-1, cols)


def reduce_heads(partial):
    nz, ny, nx = [lax.axis_size(a) for a in HEADS]
    cols = partial.shape[1]
    rows = partial.shape[0] // (nz * ny * nx)
    part = partial.reshape(nz, ny * nx, rows, cols).transpose(1, 0, 2, 3)
    part = lax.all_to_all(part, ("hy", "hx"), 0, 0, tiled=False)
    total = jnp.sum(part.astype(jnp.float32), 0)
    part = lax.all_to_all(total.astype(jnp.bfloat16), "hz", 0, 0, tiled=False)
    return jnp.sum(part.astype(jnp.float32), 0)


def on_device(
    states,
    segment_ids,
    attn_gain,
    attn_shift,
    mlp_gain,
    mlp_shift,
    qkv_weight,
    qkv_bias,
    dense_weight,
    dense_bias,
    up_weight,
    up_bias,
    down_weight,
    down_bias,
):
    floats = states.astype(jnp.float32)
    nz = lax.axis_size("hz")
    z = lax.axis_index("hz")
    swaps = [lax.ppermute(states, "hz", [(i, (i + k) % nz) for i in range(nz)]) for k in range(1, nz)]
    local = jnp.stack([jnp.sum(floats, -1), jnp.sum(floats * floats, -1)])
    every = lax.all_gather(local, HEADS + WIDTH, axis=0, tiled=False)
    heads_total = every.shape[0] // lax.axis_size(WIDTH)
    stats = jnp.sum(every.reshape(heads_total, -1, 2, local.shape[1]), 1)
    stats = stats.transpose(1, 0, 2).reshape(2, -1)
    pair = jnp.stack([states] + swaps)
    by_z = jnp.take(pair, (z - jnp.arange(nz)) % nz, axis=0)
    qkv_cols = qkv_weight.shape[1]
    heads_dev = qkv_cols // (3 * HD)
    raw_rows = gather_heads(by_z.reshape(-1, by_z.shape[2])).astype(jnp.float32)
    row_mean = (stats[0] / D)[:, None]
    row_var = (stats[1] / D)[:, None] - row_mean * row_mean
    normed = ((raw_rows - row_mean) * lax.rsqrt(row_var + norm_epsilon)).astype(jnp.bfloat16)
    block_f = normed.astype(jnp.float32)
    attn_in = (block_f * attn_gain + attn_shift).astype(jnp.bfloat16)
    mlp_in = (block_f * mlp_gain + mlp_shift).astype(jnp.bfloat16)
    projected = jnp.concatenate(
        [
            jnp.dot(attn_in, qkv_weight, preferred_element_type=jnp.float32),
            jnp.dot(mlp_in, up_weight, preferred_element_type=jnp.float32),
        ],
        axis=1,
    )
    summed_proj = lax.psum(projected.astype(jnp.bfloat16), WIDTH)
    all_tokens = projected.shape[0]
    own_rows = all_tokens // lax.axis_size(WIDTH)
    row_zero = lax.axis_index(WIDTH) * own_rows
    positions = positions_of(segment_ids)
    own_segments = lax.dynamic_slice_in_dim(segment_ids, row_zero, own_rows)
    own_index = row_zero + jnp.arange(own_rows, dtype=jnp.int32)
    score_scale = 1.0 / HD**0.5
    own_positions = lax.dynamic_slice_in_dim(positions, row_zero, own_rows)
    shaped = (summed_proj[:, :qkv_cols].astype(jnp.float32) + qkv_bias).reshape(all_tokens, heads_dev, 3, HD)
    own_shaped = lax.dynamic_slice_in_dim(shaped, row_zero, own_rows)
    queries = rotary(own_shaped[:, :, 0, :], own_positions).astype(jnp.bfloat16)
    key_heads = rotary(shaped[:, :, 1, :], positions).astype(jnp.bfloat16)
    value_heads = shaped[:, :, 2, :].astype(jnp.bfloat16)
    width_cols = heads_dev * HD
    key_cache = lax.dynamic_slice_in_dim(key_heads, row_zero, own_rows).reshape(-1, width_cols)
    value_cache = lax.dynamic_slice_in_dim(value_heads, row_zero, own_rows).reshape(-1, width_cols)
    run_max = jnp.full((heads_dev, own_rows), -1e30, jnp.float32)
    count = all_tokens
    scores = (
        jnp.einsum("rhd,nhd->hrn", queries, key_heads, preferred_element_type=jnp.float32)
        * score_scale
    )
    key_index = jnp.arange(count, dtype=jnp.int32)
    allowed = (own_segments[:, None] == segment_ids[None, :]) & (
        key_index[None, :] <= own_index[:, None]
    )
    scores = jnp.where(allowed[None], scores, -1e30)
    new_max = jnp.maximum(run_max, jnp.max(scores, -1))
    weights = jnp.where(allowed[None], jnp.exp(scores - new_max[..., None]), 0.0)
    new_sum = jnp.sum(weights, -1)
    mixed = jnp.einsum(
        "hrn,nhd->hrd",
        weights.astype(jnp.bfloat16),
        value_heads,
        preferred_element_type=jnp.float32,
    )
    attended = (
        (mixed / new_sum[..., None])
        .transpose(1, 0, 2)
        .reshape(own_rows, heads_dev * HD)
        .astype(jnp.bfloat16)
    )
    attn_part = jnp.dot(
        lax.all_gather(attended, WIDTH, axis=0, tiled=True),
        dense_weight,
        preferred_element_type=jnp.float32,
    )
    hidden = jax.nn.gelu(summed_proj[:, qkv_cols:].astype(jnp.float32) + up_bias, approximate=False).astype(
        jnp.bfloat16
    )
    hidden = lax.optimization_barrier(hidden)
    mlp_part = jnp.dot(hidden, down_weight, preferred_element_type=jnp.float32)
    summed = reduce_heads((attn_part + mlp_part).astype(jnp.bfloat16))
    layer_out = (floats + summed + dense_bias + down_bias).astype(jnp.bfloat16)
    return (layer_out, key_cache, value_cache)


def solution(mesh):
    devices = mesh.devices.reshape(2, 4, 4, 4, 2)
    fine = jax.sharding.Mesh(devices, HEADS + WIDTH)
    in_specs = (
        P(HEADS, WIDTH),
        P(),
        P(WIDTH),
        P(WIDTH),
        P(WIDTH),
        P(WIDTH),
        P(WIDTH, HEADS),
        P(HEADS),
        P(HEADS, WIDTH),
        P(WIDTH),
        P(WIDTH, HEADS),
        P(HEADS),
        P(HEADS, WIDTH),
        P(WIDTH),
    )
    out_specs = (P(HEADS, WIDTH), P(WIDTH, HEADS), P(WIDTH, HEADS))
    return jax.shard_map(
        on_device, mesh=fine, in_specs=in_specs, out_specs=out_specs, check_vma=False
    )
```

```python
import jax
import jax.numpy as jnp
from jax import lax
from jax.sharding import PartitionSpec as P

HD = 96
ROT = 24
D = 6144


norm_epsilon = 1e-05


def positions_of(segments):
    count = segments.shape[0]
    row_index = jnp.arange(count, dtype=jnp.int32)
    change = jnp.concatenate([jnp.ones((1,), bool), segments[1:] != segments[:-1]])
    first = lax.cummax(jnp.where(change, row_index, 0), axis=0)
    return (row_index - first).astype(jnp.float32)


def rotary(values, positions):
    half_rot = ROT // 2
    inverse = 10000.0 ** (-(jnp.arange(half_rot, dtype=jnp.float32) * 2.0 / ROT))
    angles = positions[:, None] * inverse[None, :]
    cosine = jnp.cos(angles)[:, None, :]
    sine_part = jnp.sin(angles)[:, None, :]
    first_half = values[..., :half_rot]
    second_half = values[..., half_rot:ROT]
    return jnp.concatenate(
        [
            first_half * cosine - second_half * sine_part,
            second_half * cosine + first_half * sine_part,
            values[..., ROT:],
        ],
        axis=-1,
    )


HEADS = ("hz", "hy", "hx")
WIDTH = ("wz", "wc")


def gather_heads(block):
    rows, cols = block.shape
    ny, nx = lax.axis_size("hy"), lax.axis_size("hx")
    spread = jnp.broadcast_to(block[None], (ny * nx,) + block.shape)
    block = lax.all_to_all(spread, ("hy", "hx"), 0, 0, tiled=False)
    nz = lax.axis_size("hz")
    block = block.reshape(ny, nx, nz, rows // nz, cols).transpose(2, 0, 1, 3, 4)
    return block.reshape(-1, cols)


def reduce_heads(partial):
    nz, ny, nx = [lax.axis_size(a) for a in HEADS]
    cols = partial.shape[1]
    rows = partial.shape[0] // (nz * ny * nx)
    part = partial.reshape(nz, ny * nx, rows, cols).transpose(1, 0, 2, 3)
    part = lax.all_to_all(part, ("hy", "hx"), 0, 0, tiled=False)
    total = jnp.sum(part.astype(jnp.float32), 0)
    part = lax.all_to_all(total.astype(jnp.bfloat16), "hz", 0, 0, tiled=False)
    return jnp.sum(part.astype(jnp.float32), 0)


def on_device(
    states,
    segment_ids,
    attn_gain,
    attn_shift,
    mlp_gain,
    mlp_shift,
    qkv_weight,
    qkv_bias,
    dense_weight,
    dense_bias,
    up_weight,
    up_bias,
    down_weight,
    down_bias,
):
    floats = states.astype(jnp.float32)
    nz = lax.axis_size("hz")
    z = lax.axis_index("hz")
    swaps = [lax.ppermute(states, "hz", [(i, (i + k) % nz) for i in range(nz)]) for k in range(1, nz)]
    local = jnp.stack([jnp.sum(floats, -1), jnp.sum(floats * floats, -1)])
    every = lax.all_gather(local, ("hz",) + WIDTH, axis=0, tiled=False)
    stats = jnp.sum(every.reshape(nz, -1, 2, local.shape[1]), 1)
    pair = jnp.stack([states] + swaps)
    by_z = jnp.take(pair, (z - jnp.arange(nz)) % nz, axis=0).astype(jnp.float32)
    row_mean = (stats[:, 0] / D)[..., None]
    row_var = (stats[:, 1] / D)[..., None] - row_mean * row_mean
    normed = ((by_z - row_mean) * lax.rsqrt(row_var + norm_epsilon)).astype(jnp.bfloat16)
    qkv_cols = qkv_weight.shape[1]
    heads_dev = qkv_cols // (3 * HD)
    block_f = gather_heads(normed.reshape(-1, normed.shape[2])).astype(jnp.float32)
    attn_in = (block_f * attn_gain + attn_shift).astype(jnp.bfloat16)
    mlp_in = (block_f * mlp_gain + mlp_shift).astype(jnp.bfloat16)
    projected = jnp.concatenate(
        [
            jnp.dot(attn_in, qkv_weight, preferred_element_type=jnp.float32),
            jnp.dot(mlp_in, up_weight, preferred_element_type=jnp.float32),
        ],
        axis=1,
    )
    summed_proj = lax.psum(projected.astype(jnp.bfloat16), WIDTH)
    all_tokens = projected.shape[0]
    own_rows = all_tokens // lax.axis_size(WIDTH)
    row_zero = lax.axis_index(WIDTH) * own_rows
    positions = positions_of(segment_ids)
    own_segments = lax.dynamic_slice_in_dim(segment_ids, row_zero, own_rows)
    own_index = row_zero + jnp.arange(own_rows, dtype=jnp.int32)
    score_scale = 1.0 / HD**0.5
    own_positions = lax.dynamic_slice_in_dim(positions, row_zero, own_rows)
    shaped = (summed_proj[:, :qkv_cols].astype(jnp.float32) + qkv_bias).reshape(all_tokens, heads_dev, 3, HD)
    own_shaped = lax.dynamic_slice_in_dim(shaped, row_zero, own_rows)
    queries = rotary(own_shaped[:, :, 0, :], own_positions).astype(jnp.bfloat16)
    key_heads = rotary(shaped[:, :, 1, :], positions).astype(jnp.bfloat16)
    value_heads = shaped[:, :, 2, :].astype(jnp.bfloat16)
    width_cols = heads_dev * HD
    key_cache = lax.dynamic_slice_in_dim(key_heads, row_zero, own_rows).reshape(-1, width_cols)
    value_cache = lax.dynamic_slice_in_dim(value_heads, row_zero, own_rows).reshape(-1, width_cols)
    run_max = jnp.full((heads_dev, own_rows), -1e30, jnp.float32)
    count = all_tokens
    scores = (
        jnp.einsum("rhd,nhd->hrn", queries, key_heads, preferred_element_type=jnp.float32)
        * score_scale
    )
    key_index = jnp.arange(count, dtype=jnp.int32)
    allowed = (own_segments[:, None] == segment_ids[None, :]) & (
        key_index[None, :] <= own_index[:, None]
    )
    scores = jnp.where(allowed[None], scores, -1e30)
    new_max = jnp.maximum(run_max, jnp.max(scores, -1))
    weights = jnp.where(allowed[None], jnp.exp(scores - new_max[..., None]), 0.0)
    new_sum = jnp.sum(weights, -1)
    mixed = jnp.einsum(
        "hrn,nhd->hrd",
        weights.astype(jnp.bfloat16),
        value_heads,
        preferred_element_type=jnp.float32,
    )
    attended = (
        (mixed / new_sum[..., None])
        .transpose(1, 0, 2)
        .reshape(own_rows, heads_dev * HD)
        .astype(jnp.bfloat16)
    )
    attn_part = jnp.dot(
        lax.all_to_all(
            jnp.broadcast_to(attended[None], (lax.axis_size(WIDTH),) + attended.shape),
            WIDTH,
            0,
            0,
            tiled=False,
        ).reshape(-1, attended.shape[1]),
        dense_weight,
        preferred_element_type=jnp.float32,
    )
    hidden = jax.nn.gelu(summed_proj[:, qkv_cols:].astype(jnp.float32) + up_bias, approximate=False).astype(
        jnp.bfloat16
    )
    hidden = lax.optimization_barrier(hidden)
    mlp_part = jnp.dot(hidden, down_weight, preferred_element_type=jnp.float32)
    summed = reduce_heads((attn_part + mlp_part).astype(jnp.bfloat16))
    layer_out = (floats + summed + dense_bias + down_bias).astype(jnp.bfloat16)
    return (layer_out, key_cache, value_cache)


def solution(mesh):
    devices = mesh.devices.reshape(2, 4, 4, 4, 2)
    fine = jax.sharding.Mesh(devices, HEADS + WIDTH)
    in_specs = (
        P(HEADS, WIDTH),
        P(),
        P(WIDTH),
        P(WIDTH),
        P(WIDTH),
        P(WIDTH),
        P(WIDTH, HEADS),
        P(HEADS),
        P(HEADS, WIDTH),
        P(WIDTH),
        P(WIDTH, HEADS),
        P(HEADS),
        P(HEADS, WIDTH),
        P(WIDTH),
    )
    out_specs = (P(HEADS, WIDTH), P(WIDTH, HEADS), P(WIDTH, HEADS))
    return jax.shard_map(
        on_device, mesh=fine, in_specs=in_specs, out_specs=out_specs, check_vma=False
    )
```

```python
import jax
import jax.numpy as jnp
from jax import lax
from jax.sharding import PartitionSpec as P

HD = 96
ROT = 24
D = 6144


norm_epsilon = 1e-05


def positions_of(segments):
    count = segments.shape[0]
    row_index = jnp.arange(count, dtype=jnp.int32)
    change = jnp.concatenate([jnp.ones((1,), bool), segments[1:] != segments[:-1]])
    first = lax.cummax(jnp.where(change, row_index, 0), axis=0)
    return (row_index - first).astype(jnp.float32)


def rotary(values, positions):
    half_rot = ROT // 2
    inverse = 10000.0 ** (-(jnp.arange(half_rot, dtype=jnp.float32) * 2.0 / ROT))
    angles = positions[:, None] * inverse[None, :]
    cosine = jnp.cos(angles)[:, None, :]
    sine_part = jnp.sin(angles)[:, None, :]
    first_half = values[..., :half_rot]
    second_half = values[..., half_rot:ROT]
    return jnp.concatenate(
        [
            first_half * cosine - second_half * sine_part,
            second_half * cosine + first_half * sine_part,
            values[..., ROT:],
        ],
        axis=-1,
    )


HEADS = ("hz", "hy", "hx")
WIDTH = ("wz", "wc")


def gather_heads(block):
    rows, cols = block.shape
    ny, nx = lax.axis_size("hy"), lax.axis_size("hx")
    spread = jnp.broadcast_to(block[None], (ny * nx,) + block.shape)
    block = lax.all_to_all(spread, ("hy", "hx"), 0, 0, tiled=False)
    nz = lax.axis_size("hz")
    block = block.reshape(ny, nx, nz, rows // nz, cols).transpose(2, 0, 1, 3, 4)
    return block.reshape(-1, cols)


def reduce_heads(partial):
    nz, ny, nx = [lax.axis_size(a) for a in HEADS]
    cols = partial.shape[1]
    rows = partial.shape[0] // (nz * ny * nx)
    part = partial.reshape(nz, ny * nx, rows, cols).transpose(1, 0, 2, 3)
    part = lax.all_to_all(part, ("hy", "hx"), 0, 0, tiled=False)
    total = jnp.sum(part.astype(jnp.float32), 0)
    part = lax.all_to_all(total.astype(jnp.bfloat16), "hz", 0, 0, tiled=False)
    return jnp.sum(part.astype(jnp.float32), 0)


def on_device(
    states,
    segment_ids,
    attn_gain,
    attn_shift,
    mlp_gain,
    mlp_shift,
    qkv_weight,
    qkv_bias,
    dense_weight,
    dense_bias,
    up_weight,
    up_bias,
    down_weight,
    down_bias,
):
    floats = states.astype(jnp.float32)
    nz = lax.axis_size("hz")
    z = lax.axis_index("hz")
    swaps = [lax.ppermute(states, "hz", [(i, (i + k) % nz) for i in range(nz)]) for k in range(1, nz)]
    local = jnp.stack([jnp.sum(floats, -1), jnp.sum(floats * floats, -1)])
    group = nz * lax.axis_size(WIDTH)
    every = lax.all_to_all(
        jnp.broadcast_to(local[None], (group,) + local.shape), ("hz",) + WIDTH, 0, 0, tiled=False
    )
    stats = jnp.sum(every.reshape(nz, -1, 2, local.shape[1]), 1)
    pair = jnp.stack([states] + swaps)
    by_z = jnp.take(pair, (z - jnp.arange(nz)) % nz, axis=0).astype(jnp.float32)
    row_mean = (stats[:, 0] / D)[..., None]
    row_var = (stats[:, 1] / D)[..., None] - row_mean * row_mean
    normed = ((by_z - row_mean) * lax.rsqrt(row_var + norm_epsilon)).astype(jnp.bfloat16)
    qkv_cols = qkv_weight.shape[1]
    heads_dev = qkv_cols // (3 * HD)
    block_f = gather_heads(normed.reshape(-1, normed.shape[2])).astype(jnp.float32)
    attn_in = (block_f * attn_gain + attn_shift).astype(jnp.bfloat16)
    mlp_in = (block_f * mlp_gain + mlp_shift).astype(jnp.bfloat16)
    projected = jnp.concatenate(
        [
            jnp.dot(attn_in, qkv_weight, preferred_element_type=jnp.float32),
            jnp.dot(mlp_in, up_weight, preferred_element_type=jnp.float32),
        ],
        axis=1,
    )
    summed_proj = lax.psum(projected.astype(jnp.bfloat16), WIDTH)
    all_tokens = projected.shape[0]
    own_rows = all_tokens // lax.axis_size(WIDTH)
    row_zero = lax.axis_index(WIDTH) * own_rows
    positions = positions_of(segment_ids)
    own_segments = lax.dynamic_slice_in_dim(segment_ids, row_zero, own_rows)
    own_index = row_zero + jnp.arange(own_rows, dtype=jnp.int32)
    score_scale = 1.0 / HD**0.5
    own_positions = lax.dynamic_slice_in_dim(positions, row_zero, own_rows)
    shaped = (summed_proj[:, :qkv_cols].astype(jnp.float32) + qkv_bias).reshape(all_tokens, heads_dev, 3, HD)
    own_shaped = lax.dynamic_slice_in_dim(shaped, row_zero, own_rows)
    queries = rotary(own_shaped[:, :, 0, :], own_positions).astype(jnp.bfloat16)
    key_heads = rotary(shaped[:, :, 1, :], positions).astype(jnp.bfloat16)
    value_heads = shaped[:, :, 2, :].astype(jnp.bfloat16)
    width_cols = heads_dev * HD
    key_cache = lax.dynamic_slice_in_dim(key_heads, row_zero, own_rows).reshape(-1, width_cols)
    value_cache = lax.dynamic_slice_in_dim(value_heads, row_zero, own_rows).reshape(-1, width_cols)
    run_max = jnp.full((heads_dev, own_rows), -1e30, jnp.float32)
    count = all_tokens
    scores = (
        jnp.einsum("rhd,nhd->hrn", queries, key_heads, preferred_element_type=jnp.float32)
        * score_scale
    )
    key_index = jnp.arange(count, dtype=jnp.int32)
    allowed = (own_segments[:, None] == segment_ids[None, :]) & (
        key_index[None, :] <= own_index[:, None]
    )
    scores = jnp.where(allowed[None], scores, -1e30)
    new_max = jnp.maximum(run_max, jnp.max(scores, -1))
    weights = jnp.where(allowed[None], jnp.exp(scores - new_max[..., None]), 0.0)
    new_sum = jnp.sum(weights, -1)
    mixed = jnp.einsum(
        "hrn,nhd->hrd",
        weights.astype(jnp.bfloat16),
        value_heads,
        preferred_element_type=jnp.float32,
    )
    attended = (
        (mixed / new_sum[..., None])
        .transpose(1, 0, 2)
        .reshape(own_rows, heads_dev * HD)
        .astype(jnp.bfloat16)
    )
    attn_part = jnp.dot(
        lax.all_to_all(
            jnp.broadcast_to(attended[None], (lax.axis_size(WIDTH),) + attended.shape),
            WIDTH,
            0,
            0,
            tiled=False,
        ).reshape(-1, attended.shape[1]),
        dense_weight,
        preferred_element_type=jnp.float32,
    )
    hidden = jax.nn.gelu(summed_proj[:, qkv_cols:].astype(jnp.float32) + up_bias, approximate=False).astype(
        jnp.bfloat16
    )
    hidden = lax.optimization_barrier(hidden)
    mlp_part = jnp.dot(hidden, down_weight, preferred_element_type=jnp.float32)
    summed = reduce_heads((attn_part + mlp_part).astype(jnp.bfloat16))
    layer_out = (floats + summed + dense_bias + down_bias).astype(jnp.bfloat16)
    return (layer_out, key_cache, value_cache)


def solution(mesh):
    devices = mesh.devices.reshape(2, 4, 4, 4, 2)
    fine = jax.sharding.Mesh(devices, HEADS + WIDTH)
    in_specs = (
        P(HEADS, WIDTH),
        P(),
        P(WIDTH),
        P(WIDTH),
        P(WIDTH),
        P(WIDTH),
        P(WIDTH, HEADS),
        P(HEADS),
        P(HEADS, WIDTH),
        P(WIDTH),
        P(WIDTH, HEADS),
        P(HEADS),
        P(HEADS, WIDTH),
        P(WIDTH),
    )
    out_specs = (P(HEADS, WIDTH), P(WIDTH, HEADS), P(WIDTH, HEADS))
    return jax.shard_map(
        on_device, mesh=fine, in_specs=in_specs, out_specs=out_specs, check_vma=False
    )
```

```python
import jax
import jax.numpy as jnp
from jax import lax
from jax.sharding import PartitionSpec as P

HD = 96
ROT = 24
D = 6144


norm_epsilon = 1e-05


def positions_of(segments):
    count = segments.shape[0]
    row_index = jnp.arange(count, dtype=jnp.int32)
    change = jnp.concatenate([jnp.ones((1,), bool), segments[1:] != segments[:-1]])
    first = lax.cummax(jnp.where(change, row_index, 0), axis=0)
    return (row_index - first).astype(jnp.float32)


def rotary(values, positions):
    half_rot = ROT // 2
    inverse = 10000.0 ** (-(jnp.arange(half_rot, dtype=jnp.float32) * 2.0 / ROT))
    angles = positions[:, None] * inverse[None, :]
    cosine = jnp.cos(angles)[:, None, :]
    sine_part = jnp.sin(angles)[:, None, :]
    first_half = values[..., :half_rot]
    second_half = values[..., half_rot:ROT]
    return jnp.concatenate(
        [
            first_half * cosine - second_half * sine_part,
            second_half * cosine + first_half * sine_part,
            values[..., ROT:],
        ],
        axis=-1,
    )


HEADS = ("hz", "hy", "hx")
WIDTH = ("wz", "wc")


def gather_heads(block):
    rows, cols = block.shape
    ny, nx = lax.axis_size("hy"), lax.axis_size("hx")
    spread = jnp.broadcast_to(block[None], (ny * nx,) + block.shape)
    block = lax.all_to_all(spread, ("hy", "hx"), 0, 0, tiled=False)
    nz = lax.axis_size("hz")
    block = block.reshape(ny, nx, nz, rows // nz, cols).transpose(2, 0, 1, 3, 4)
    return block.reshape(-1, cols)


def reduce_heads(partial):
    nz, ny, nx = [lax.axis_size(a) for a in HEADS]
    cols = partial.shape[1]
    rows = partial.shape[0] // (nz * ny * nx)
    part = partial.reshape(nz, ny * nx, rows, cols).transpose(1, 0, 2, 3)
    part = lax.all_to_all(part, ("hy", "hx"), 0, 0, tiled=False)
    total = jnp.sum(part.astype(jnp.float32), 0)
    part = lax.all_to_all(total.astype(jnp.bfloat16), "hz", 0, 0, tiled=False)
    return jnp.sum(part.astype(jnp.float32), 0)


def on_device(
    states,
    segment_ids,
    attn_gain,
    attn_shift,
    mlp_gain,
    mlp_shift,
    qkv_weight,
    qkv_bias,
    dense_weight,
    dense_bias,
    up_weight,
    up_bias,
    down_weight,
    down_bias,
):
    floats = states.astype(jnp.float32)
    nz = lax.axis_size("hz")
    z = lax.axis_index("hz")
    swaps = [lax.ppermute(states, "hz", [(i, (i + k) % nz) for i in range(nz)]) for k in range(1, nz)]
    local = jnp.stack([jnp.sum(floats, -1), jnp.sum(floats * floats, -1)])
    group = nz * lax.axis_size(WIDTH)
    every = lax.all_to_all(
        jnp.broadcast_to(local[None], (group,) + local.shape), ("hz",) + WIDTH, 0, 0, tiled=False
    )
    stats = jnp.sum(every.reshape(nz, -1, 2, local.shape[1]), 1)
    pair = jnp.stack([states] + swaps)
    by_z = jnp.take(pair, (z - jnp.arange(nz)) % nz, axis=0).astype(jnp.float32)
    row_mean = (stats[:, 0] / D)[..., None]
    row_var = (stats[:, 1] / D)[..., None] - row_mean * row_mean
    normed = ((by_z - row_mean) * lax.rsqrt(row_var + norm_epsilon)).astype(jnp.bfloat16)
    qkv_cols = qkv_weight.shape[1]
    heads_dev = qkv_cols // (3 * HD)
    block_f = gather_heads(normed.reshape(-1, normed.shape[2])).astype(jnp.float32)
    attn_in = (block_f * attn_gain + attn_shift).astype(jnp.bfloat16)
    mlp_in = (block_f * mlp_gain + mlp_shift).astype(jnp.bfloat16)
    projected = jnp.concatenate(
        [
            jnp.dot(attn_in, qkv_weight, preferred_element_type=jnp.float32),
            jnp.dot(mlp_in, up_weight, preferred_element_type=jnp.float32),
        ],
        axis=1,
    )
    summed_proj = lax.psum(projected.astype(jnp.bfloat16), WIDTH)
    all_tokens = projected.shape[0]
    own_rows = all_tokens // lax.axis_size(WIDTH)
    row_zero = lax.axis_index(WIDTH) * own_rows
    positions = positions_of(segment_ids)
    own_segments = lax.dynamic_slice_in_dim(segment_ids, row_zero, own_rows)
    own_index = row_zero + jnp.arange(own_rows, dtype=jnp.int32)
    score_scale = 1.0 / HD**0.5
    own_positions = lax.dynamic_slice_in_dim(positions, row_zero, own_rows)
    shaped = (summed_proj[:, :qkv_cols].astype(jnp.float32) + qkv_bias).reshape(all_tokens, heads_dev, 3, HD)
    own_shaped = lax.dynamic_slice_in_dim(shaped, row_zero, own_rows)
    queries = rotary(own_shaped[:, :, 0, :], own_positions).astype(jnp.bfloat16)
    key_heads = rotary(shaped[:, :, 1, :], positions).astype(jnp.bfloat16)
    value_heads = shaped[:, :, 2, :].astype(jnp.bfloat16)
    width_cols = heads_dev * HD
    key_cache = lax.dynamic_slice_in_dim(key_heads, row_zero, own_rows).reshape(-1, width_cols)
    value_cache = lax.dynamic_slice_in_dim(value_heads, row_zero, own_rows).reshape(-1, width_cols)
    run_max = jnp.full((heads_dev, own_rows), -1e30, jnp.float32)
    count = all_tokens
    scores = (
        jnp.einsum("rhd,nhd->hrn", queries, key_heads, preferred_element_type=jnp.float32)
        * score_scale
    )
    key_index = jnp.arange(count, dtype=jnp.int32)
    allowed = (own_segments[:, None] == segment_ids[None, :]) & (
        key_index[None, :] <= own_index[:, None]
    )
    scores = jnp.where(allowed[None], scores, -1e30)
    new_max = jnp.maximum(run_max, jnp.max(scores, -1))
    weights = jnp.where(allowed[None], jnp.exp(scores - new_max[..., None]), 0.0)
    new_sum = jnp.sum(weights, -1)
    mixed = jnp.einsum(
        "hrn,nhd->hrd",
        weights.astype(jnp.bfloat16),
        value_heads,
        preferred_element_type=jnp.float32,
    )
    attended = (
        (mixed / new_sum[..., None])
        .transpose(1, 0, 2)
        .reshape(own_rows, heads_dev * HD)
        .astype(jnp.bfloat16)
    )
    gathered = lax.all_to_all(
        jnp.broadcast_to(attended[None], (lax.axis_size(WIDTH),) + attended.shape),
        WIDTH,
        0,
        0,
        tiled=False,
    ).reshape(-1, attended.shape[1])
    hidden = jax.nn.gelu(summed_proj[:, qkv_cols:].astype(jnp.float32) + up_bias, approximate=False).astype(
        jnp.bfloat16
    )
    hidden = lax.optimization_barrier(hidden)
    half = dense_weight.shape[1] // 2
    halves = []
    for cols in (slice(0, half), slice(half, None)):
        attn_part = jnp.dot(gathered, dense_weight[:, cols], preferred_element_type=jnp.float32)
        mlp_part = jnp.dot(hidden, down_weight[:, cols], preferred_element_type=jnp.float32)
        halves.append(reduce_heads((attn_part + mlp_part).astype(jnp.bfloat16)))
    summed = jnp.concatenate(halves, axis=1)
    layer_out = (floats + summed + dense_bias + down_bias).astype(jnp.bfloat16)
    return (layer_out, key_cache, value_cache)


def solution(mesh):
    devices = mesh.devices.reshape(2, 4, 4, 4, 2)
    fine = jax.sharding.Mesh(devices, HEADS + WIDTH)
    in_specs = (
        P(HEADS, WIDTH),
        P(),
        P(WIDTH),
        P(WIDTH),
        P(WIDTH),
        P(WIDTH),
        P(WIDTH, HEADS),
        P(HEADS),
        P(HEADS, WIDTH),
        P(WIDTH),
        P(WIDTH, HEADS),
        P(HEADS),
        P(HEADS, WIDTH),
        P(WIDTH),
    )
    out_specs = (P(HEADS, WIDTH), P(WIDTH, HEADS), P(WIDTH, HEADS))
    return jax.shard_map(
        on_device, mesh=fine, in_specs=in_specs, out_specs=out_specs, check_vma=False
    )
```

```python
import jax
import jax.numpy as jnp
from jax import lax
from jax.sharding import PartitionSpec as P

HD = 96
ROT = 24
D = 6144


norm_epsilon = 1e-05


def positions_of(segments):
    count = segments.shape[0]
    row_index = jnp.arange(count, dtype=jnp.int32)
    change = jnp.concatenate([jnp.ones((1,), bool), segments[1:] != segments[:-1]])
    first = lax.cummax(jnp.where(change, row_index, 0), axis=0)
    return (row_index - first).astype(jnp.float32)


def rotary(values, positions):
    half_rot = ROT // 2
    inverse = 10000.0 ** (-(jnp.arange(half_rot, dtype=jnp.float32) * 2.0 / ROT))
    angles = positions[:, None] * inverse[None, :]
    cosine = jnp.cos(angles)[:, None, :]
    sine_part = jnp.sin(angles)[:, None, :]
    first_half = values[..., :half_rot]
    second_half = values[..., half_rot:ROT]
    return jnp.concatenate(
        [
            first_half * cosine - second_half * sine_part,
            second_half * cosine + first_half * sine_part,
            values[..., ROT:],
        ],
        axis=-1,
    )


HEADS = ("hz", "hy", "hx")
WIDTH = ("wz", "wc")


def gather_heads(block):
    rows, cols = block.shape
    ny, nx = lax.axis_size("hy"), lax.axis_size("hx")
    spread = jnp.broadcast_to(block[None], (ny * nx,) + block.shape)
    block = lax.all_to_all(spread, ("hy", "hx"), 0, 0, tiled=False)
    nz = lax.axis_size("hz")
    block = block.reshape(ny, nx, nz, rows // nz, cols).transpose(2, 0, 1, 3, 4)
    return block.reshape(-1, cols)


def reduce_heads(partial):
    nz, ny, nx = [lax.axis_size(a) for a in HEADS]
    cols = partial.shape[1]
    rows = partial.shape[0] // (nz * ny * nx)
    part = partial.reshape(nz, ny * nx, rows, cols).transpose(1, 0, 2, 3)
    part = lax.all_to_all(part, ("hy", "hx"), 0, 0, tiled=False)
    total = jnp.sum(part.astype(jnp.float32), 0)
    part = lax.all_to_all(total.astype(jnp.bfloat16), "hz", 0, 0, tiled=False)
    return jnp.sum(part.astype(jnp.float32), 0)


def on_device(
    states,
    segment_ids,
    attn_gain,
    attn_shift,
    mlp_gain,
    mlp_shift,
    qkv_weight,
    qkv_bias,
    dense_weight,
    dense_bias,
    up_weight,
    up_bias,
    down_weight,
    down_bias,
):
    floats = states.astype(jnp.float32)
    nz = lax.axis_size("hz")
    z = lax.axis_index("hz")
    swaps = [lax.ppermute(states, "hz", [(i, (i + k) % nz) for i in range(nz)]) for k in range(1, nz)]
    local = jnp.stack([jnp.sum(floats, -1), jnp.sum(floats * floats, -1)])
    group = nz * lax.axis_size(WIDTH)
    every = lax.all_to_all(
        jnp.broadcast_to(local[None], (group,) + local.shape), ("hz",) + WIDTH, 0, 0, tiled=False
    )
    stats = jnp.sum(every.reshape(nz, -1, 2, local.shape[1]), 1)
    pair = jnp.stack([states] + swaps)
    by_z = jnp.take(pair, (z - jnp.arange(nz)) % nz, axis=0).astype(jnp.float32)
    row_mean = (stats[:, 0] / D)[..., None]
    row_var = (stats[:, 1] / D)[..., None] - row_mean * row_mean
    normed = ((by_z - row_mean) * lax.rsqrt(row_var + norm_epsilon)).astype(jnp.bfloat16)
    qkv_cols = qkv_weight.shape[1]
    heads_dev = qkv_cols // (3 * HD)
    block_f = gather_heads(normed.reshape(-1, normed.shape[2])).astype(jnp.float32)
    attn_in = (block_f * attn_gain + attn_shift).astype(jnp.bfloat16)
    mlp_in = (block_f * mlp_gain + mlp_shift).astype(jnp.bfloat16)
    qkv_sum, up_sum = lax.psum(
        (
            jnp.dot(attn_in, qkv_weight, preferred_element_type=jnp.float32).astype(jnp.bfloat16),
            jnp.dot(mlp_in, up_weight, preferred_element_type=jnp.float32).astype(jnp.bfloat16),
        ),
        WIDTH,
    )
    all_tokens = qkv_sum.shape[0]
    own_rows = all_tokens // lax.axis_size(WIDTH)
    row_zero = lax.axis_index(WIDTH) * own_rows
    positions = positions_of(segment_ids)
    own_segments = lax.dynamic_slice_in_dim(segment_ids, row_zero, own_rows)
    own_index = row_zero + jnp.arange(own_rows, dtype=jnp.int32)
    score_scale = 1.0 / HD**0.5
    own_positions = lax.dynamic_slice_in_dim(positions, row_zero, own_rows)
    shaped = (qkv_sum.astype(jnp.float32) + qkv_bias).reshape(all_tokens, heads_dev, 3, HD)
    own_shaped = lax.dynamic_slice_in_dim(shaped, row_zero, own_rows)
    queries = rotary(own_shaped[:, :, 0, :], own_positions).astype(jnp.bfloat16)
    key_heads = rotary(shaped[:, :, 1, :], positions).astype(jnp.bfloat16)
    value_heads = shaped[:, :, 2, :].astype(jnp.bfloat16)
    width_cols = heads_dev * HD
    key_cache = lax.dynamic_slice_in_dim(key_heads, row_zero, own_rows).reshape(-1, width_cols)
    value_cache = lax.dynamic_slice_in_dim(value_heads, row_zero, own_rows).reshape(-1, width_cols)
    run_max = jnp.full((heads_dev, own_rows), -1e30, jnp.float32)
    count = all_tokens
    scores = (
        jnp.einsum("rhd,nhd->hrn", queries, key_heads, preferred_element_type=jnp.float32)
        * score_scale
    )
    key_index = jnp.arange(count, dtype=jnp.int32)
    allowed = (own_segments[:, None] == segment_ids[None, :]) & (
        key_index[None, :] <= own_index[:, None]
    )
    scores = jnp.where(allowed[None], scores, -1e30)
    new_max = jnp.maximum(run_max, jnp.max(scores, -1))
    weights = jnp.where(allowed[None], jnp.exp(scores - new_max[..., None]), 0.0)
    new_sum = jnp.sum(weights, -1)
    mixed = jnp.einsum(
        "hrn,nhd->hrd",
        weights.astype(jnp.bfloat16),
        value_heads,
        preferred_element_type=jnp.float32,
    )
    attended = (
        (mixed / new_sum[..., None])
        .transpose(1, 0, 2)
        .reshape(own_rows, heads_dev * HD)
        .astype(jnp.bfloat16)
    )
    attn_part = jnp.dot(
        lax.all_to_all(
            jnp.broadcast_to(attended[None], (lax.axis_size(WIDTH),) + attended.shape),
            WIDTH,
            0,
            0,
            tiled=False,
        ).reshape(-1, attended.shape[1]),
        dense_weight,
        preferred_element_type=jnp.float32,
    )
    hidden = jax.nn.gelu(up_sum.astype(jnp.float32) + up_bias, approximate=False).astype(
        jnp.bfloat16
    )
    hidden = lax.optimization_barrier(hidden)
    mlp_part = jnp.dot(hidden, down_weight, preferred_element_type=jnp.float32)
    summed = reduce_heads((attn_part + mlp_part).astype(jnp.bfloat16))
    layer_out = (floats + summed + dense_bias + down_bias).astype(jnp.bfloat16)
    return (layer_out, key_cache, value_cache)


def solution(mesh):
    devices = mesh.devices.reshape(2, 4, 4, 4, 2)
    fine = jax.sharding.Mesh(devices, HEADS + WIDTH)
    in_specs = (
        P(HEADS, WIDTH),
        P(),
        P(WIDTH),
        P(WIDTH),
        P(WIDTH),
        P(WIDTH),
        P(WIDTH, HEADS),
        P(HEADS),
        P(HEADS, WIDTH),
        P(WIDTH),
        P(WIDTH, HEADS),
        P(HEADS),
        P(HEADS, WIDTH),
        P(WIDTH),
    )
    out_specs = (P(HEADS, WIDTH), P(WIDTH, HEADS), P(WIDTH, HEADS))
    return jax.shard_map(
        on_device, mesh=fine, in_specs=in_specs, out_specs=out_specs, check_vma=False
    )
```

```python
import jax
import jax.numpy as jnp
from jax import lax
from jax.sharding import PartitionSpec as P

HD = 96
ROT = 24
D = 6144


norm_epsilon = 1e-05


def positions_of(segments):
    count = segments.shape[0]
    row_index = jnp.arange(count, dtype=jnp.int32)
    change = jnp.concatenate([jnp.ones((1,), bool), segments[1:] != segments[:-1]])
    first = lax.cummax(jnp.where(change, row_index, 0), axis=0)
    return (row_index - first).astype(jnp.float32)


def rotary(values, positions):
    half_rot = ROT // 2
    inverse = 10000.0 ** (-(jnp.arange(half_rot, dtype=jnp.float32) * 2.0 / ROT))
    angles = positions[:, None] * inverse[None, :]
    cosine = jnp.cos(angles)[:, None, :]
    sine_part = jnp.sin(angles)[:, None, :]
    first_half = values[..., :half_rot]
    second_half = values[..., half_rot:ROT]
    return jnp.concatenate(
        [
            first_half * cosine - second_half * sine_part,
            second_half * cosine + first_half * sine_part,
            values[..., ROT:],
        ],
        axis=-1,
    )


HEADS = ("hz", "hy", "hx")
WIDTH = ("wz", "wc")


def gather_heads(block):
    rows, cols = block.shape
    ny, nx = lax.axis_size("hy"), lax.axis_size("hx")
    spread = jnp.broadcast_to(block[None], (ny * nx,) + block.shape)
    block = lax.all_to_all(spread, ("hy", "hx"), 0, 0, tiled=False)
    nz = lax.axis_size("hz")
    block = block.reshape(ny, nx, nz, rows // nz, cols).transpose(2, 0, 1, 3, 4)
    return block.reshape(-1, cols)


def reduce_heads(partial):
    nz, ny, nx = [lax.axis_size(a) for a in HEADS]
    cols = partial.shape[1]
    rows = partial.shape[0] // (nz * ny * nx)
    part = partial.reshape(nz, ny * nx, rows, cols).transpose(1, 0, 2, 3)
    part = lax.all_to_all(part, ("hy", "hx"), 0, 0, tiled=False)
    total = jnp.sum(part.astype(jnp.float32), 0)
    z = lax.axis_index("hz")
    result = lax.dynamic_index_in_dim(total, z, 0, keepdims=False)
    for k in range(1, nz):
        outgoing = lax.dynamic_index_in_dim(total, (z + k) % nz, 0, keepdims=False)
        incoming = lax.ppermute(
            outgoing.astype(jnp.bfloat16), "hz", [(i, (i + k) % nz) for i in range(nz)]
        )
        result = result + incoming.astype(jnp.float32)
    return result


def on_device(
    states,
    segment_ids,
    attn_gain,
    attn_shift,
    mlp_gain,
    mlp_shift,
    qkv_weight,
    qkv_bias,
    dense_weight,
    dense_bias,
    up_weight,
    up_bias,
    down_weight,
    down_bias,
):
    floats = states.astype(jnp.float32)
    nz = lax.axis_size("hz")
    z = lax.axis_index("hz")
    swaps = [lax.ppermute(states, "hz", [(i, (i + k) % nz) for i in range(nz)]) for k in range(1, nz)]
    local = jnp.stack([jnp.sum(floats, -1), jnp.sum(floats * floats, -1)])
    group = nz * lax.axis_size(WIDTH)
    every = lax.all_to_all(
        jnp.broadcast_to(local[None], (group,) + local.shape), ("hz",) + WIDTH, 0, 0, tiled=False
    )
    stats = jnp.sum(every.reshape(nz, -1, 2, local.shape[1]), 1)
    pair = jnp.stack([states] + swaps)
    by_z = jnp.take(pair, (z - jnp.arange(nz)) % nz, axis=0).astype(jnp.float32)
    row_mean = (stats[:, 0] / D)[..., None]
    row_var = (stats[:, 1] / D)[..., None] - row_mean * row_mean
    normed = ((by_z - row_mean) * lax.rsqrt(row_var + norm_epsilon)).astype(jnp.bfloat16)
    qkv_cols = qkv_weight.shape[1]
    heads_dev = qkv_cols // (3 * HD)
    block_f = gather_heads(normed.reshape(-1, normed.shape[2])).astype(jnp.float32)
    attn_in = (block_f * attn_gain + attn_shift).astype(jnp.bfloat16)
    mlp_in = (block_f * mlp_gain + mlp_shift).astype(jnp.bfloat16)
    projected = jnp.concatenate(
        [
            jnp.dot(attn_in, qkv_weight, preferred_element_type=jnp.float32),
            jnp.dot(mlp_in, up_weight, preferred_element_type=jnp.float32),
        ],
        axis=1,
    )
    summed_proj = lax.psum(projected.astype(jnp.bfloat16), WIDTH)
    all_tokens = projected.shape[0]
    own_rows = all_tokens // lax.axis_size(WIDTH)
    row_zero = lax.axis_index(WIDTH) * own_rows
    positions = positions_of(segment_ids)
    own_segments = lax.dynamic_slice_in_dim(segment_ids, row_zero, own_rows)
    own_index = row_zero + jnp.arange(own_rows, dtype=jnp.int32)
    score_scale = 1.0 / HD**0.5
    own_positions = lax.dynamic_slice_in_dim(positions, row_zero, own_rows)
    shaped = (summed_proj[:, :qkv_cols].astype(jnp.float32) + qkv_bias).reshape(all_tokens, heads_dev, 3, HD)
    own_shaped = lax.dynamic_slice_in_dim(shaped, row_zero, own_rows)
    queries = rotary(own_shaped[:, :, 0, :], own_positions).astype(jnp.bfloat16)
    key_heads = rotary(shaped[:, :, 1, :], positions).astype(jnp.bfloat16)
    value_heads = shaped[:, :, 2, :].astype(jnp.bfloat16)
    width_cols = heads_dev * HD
    key_cache = lax.dynamic_slice_in_dim(key_heads, row_zero, own_rows).reshape(-1, width_cols)
    value_cache = lax.dynamic_slice_in_dim(value_heads, row_zero, own_rows).reshape(-1, width_cols)
    run_max = jnp.full((heads_dev, own_rows), -1e30, jnp.float32)
    count = all_tokens
    scores = (
        jnp.einsum("rhd,nhd->hrn", queries, key_heads, preferred_element_type=jnp.float32)
        * score_scale
    )
    key_index = jnp.arange(count, dtype=jnp.int32)
    allowed = (own_segments[:, None] == segment_ids[None, :]) & (
        key_index[None, :] <= own_index[:, None]
    )
    scores = jnp.where(allowed[None], scores, -1e30)
    new_max = jnp.maximum(run_max, jnp.max(scores, -1))
    weights = jnp.where(allowed[None], jnp.exp(scores - new_max[..., None]), 0.0)
    new_sum = jnp.sum(weights, -1)
    mixed = jnp.einsum(
        "hrn,nhd->hrd",
        weights.astype(jnp.bfloat16),
        value_heads,
        preferred_element_type=jnp.float32,
    )
    attended = (
        (mixed / new_sum[..., None])
        .transpose(1, 0, 2)
        .reshape(own_rows, heads_dev * HD)
        .astype(jnp.bfloat16)
    )
    attn_part = jnp.dot(
        lax.all_to_all(
            jnp.broadcast_to(attended[None], (lax.axis_size(WIDTH),) + attended.shape),
            WIDTH,
            0,
            0,
            tiled=False,
        ).reshape(-1, attended.shape[1]),
        dense_weight,
        preferred_element_type=jnp.float32,
    )
    hidden = jax.nn.gelu(summed_proj[:, qkv_cols:].astype(jnp.float32) + up_bias, approximate=False).astype(
        jnp.bfloat16
    )
    hidden = lax.optimization_barrier(hidden)
    mlp_part = jnp.dot(hidden, down_weight, preferred_element_type=jnp.float32)
    summed = reduce_heads((attn_part + mlp_part).astype(jnp.bfloat16))
    layer_out = (floats + summed + dense_bias + down_bias).astype(jnp.bfloat16)
    return (layer_out, key_cache, value_cache)


def solution(mesh):
    devices = mesh.devices.reshape(2, 4, 4, 4, 2)
    fine = jax.sharding.Mesh(devices, HEADS + WIDTH)
    in_specs = (
        P(HEADS, WIDTH),
        P(),
        P(WIDTH),
        P(WIDTH),
        P(WIDTH),
        P(WIDTH),
        P(WIDTH, HEADS),
        P(HEADS),
        P(HEADS, WIDTH),
        P(WIDTH),
        P(WIDTH, HEADS),
        P(HEADS),
        P(HEADS, WIDTH),
        P(WIDTH),
    )
    out_specs = (P(HEADS, WIDTH), P(WIDTH, HEADS), P(WIDTH, HEADS))
    return jax.shard_map(
        on_device, mesh=fine, in_specs=in_specs, out_specs=out_specs, check_vma=False
    )
```
